32 devices in a mesh: groups: 2 (over x), rows: 16 (over z, y, core).
Axes of the slice: x: 2, y: 2, z: 4, core: 2. Of those that a mesh axis runs over, the one named last changes fastest.
Arguments:
- source_emb: float32 [65536, 128], P(('groups', 'rows')), parts along dimension 0, may hold values from -6 to 6
- target_emb: float32 [16384, 128], P(('groups', 'rows')), parts along dimension 0, may hold values from -6 to 6
- tile_source: int32 [4096], P(('groups', 'rows')), parts along dimension 0, may hold values from 0 to 15, as said below
- tile_slot: int32 [4096], P(('groups', 'rows')), parts along dimension 0, may hold values from 0 to 15
- tile_count: int32 [32], P(('groups', 'rows')), parts along dimension 0, may hold values from 21 to 128, as said below
- wanted: int32 [512, 1], P(('groups', 'rows')), parts along dimension 0, may hold values from 0 to 3, as said below
Outputs:
- aligned: float32 [65536, 128], P(('groups', 'rows')), parts along dimension 0
- row_mass: float32 [65536], P(('groups', 'rows')), parts along dimension 0
The draws below stay inside these ranges and needn't reach their ends.
There are 2 independent parts, one for each index of `groups`. The reference program is written for one: setup_inputs(seed, part) draws one part's arguments, and reference() takes and returns one part's arrays. A program takes and returns all parts, laid end to end along the dimension named above; each array names one. Nothing has to cross between parts.
Inputs may be any that keep to these rules, and one draw needn't show every extreme that they name: Within one device the 128 pairs (tile_source, tile_slot) are distinct, live or not. `tile_count`: some device has exactly 128 live tiles. `wanted`: the 1 block that one device requests from one owner are distinct; each owner has one block that no device requests.
All inputs are finite; a program needn't handle non-finite values.
Results may differ from the reference program's by a relative error of at most 0.0003.
Values sent between devices are 32-bit elements; how exact they have to be, the bound alone decides.
No kernel may reach another device: no remote copies, remote signals or barrier semaphores. Data moves between devices by JAX's collectives and lax.ppermute only.
A program may use at most 128 MiB of HBM per device.

```python
import math
import jax
import jax.numpy as jnp
from jax import lax

E = 128
BLOCK = 128
SB_DEV = 16
TB_DEV = 4
NEED = 1
CAP = 128
ITERS = 2
SRC = 32768
TGT = 8192
N_ROWS = 16


def draw_pairs(key):
    base = jax.random.fold_in(key, 17)
    device_keys = jax.random.split(base, N_ROWS)

    def per_device(device_key):
        return jax.random.permutation(device_key, SB_DEV * N_ROWS * NEED)[:CAP]
    chosen = jax.vmap(per_device)(device_keys)
    return chosen.reshape(-1).astype(jnp.int32)


def draw_tile_source(key, part):
    return (draw_pairs(key) // (N_ROWS * NEED)).astype(jnp.int32)


def draw_tile_slot(key, part):
    return (draw_pairs(key) % (N_ROWS * NEED)).astype(jnp.int32)


def draw_tile_count(key, part):
    leading_key, second_key = jax.random.split(jax.random.fold_in(key, 29))
    divisor = jax.random.randint(leading_key, (N_ROWS,), 1, 7)
    busiest = jax.random.randint(second_key, (), 0, N_ROWS)
    divisor = jnp.where(jnp.arange(N_ROWS) == busiest, 1, divisor)
    return (CAP // divisor).astype(jnp.int32)


def draw_wanted(key, part):
    leading_key, second_key = jax.random.split(jax.random.fold_in(key, 41))
    dangling = jax.random.randint(leading_key, (N_ROWS,), 0, TB_DEV)
    pair_keys = jax.random.split(second_key, N_ROWS * N_ROWS)

    def pick_blocks(pair_key):
        return jax.random.permutation(pair_key, TB_DEV - 1)[:NEED]
    picks = jax.vmap(pick_blocks)(pair_keys)
    owners = jnp.arange(N_ROWS * N_ROWS) % N_ROWS
    passed_over = dangling[owners][:, None]
    return jnp.where(picks >= passed_over, picks + 1, picks).astype(jnp.int32)


def level_of(rng, extent, pieces, least, high):
    gain, own = 1.0, jax.random.fold_in(rng, 6)
    for axis_at, blocks in pieces:
        draws = jnp.exp(jax.random.uniform(jax.random.fold_in(own, axis_at), (blocks,), jnp.float32, least / len(pieces), high / len(pieces)))
        gain = gain * jnp.repeat(draws, extent[axis_at] // blocks).reshape([-1 if axis == axis_at else 1 for axis in range(len(extent))])
    return gain


def bell_draw(stream_key, shape, width, bound, cuts=(), held_as=jnp.bfloat16):
    result = jax.random.normal(stream_key, shape, jnp.float32) * width
    if len(cuts) > 0:
        result = level_of(stream_key, shape, cuts, -0.22, 0.18) * result
    return jnp.clip(result, min=-bound, max=bound).astype(held_as)


def setup_inputs(seed: int = 0, part: int = 0) -> dict:
    keys = jax.random.split(jax.random.key(seed), 7)
    part_keys = jax.random.split(jax.random.fold_in(keys[6], part), 7)
    source_emb = bell_draw(part_keys[0], (SRC, E), 1.0, 6.0, ((0, 16),), jnp.float32)
    target_emb = bell_draw(part_keys[1], (TGT, E), 1.0, 6.0, ((0, 16),), jnp.float32)
    tile_source = draw_tile_source(jax.random.fold_in(jax.random.fold_in(keys[6], part), 71), part)
    tile_slot = draw_tile_slot(jax.random.fold_in(jax.random.fold_in(keys[6], part), 71), part)
    tile_count = draw_tile_count(jax.random.fold_in(jax.random.fold_in(keys[6], part), 71), part)
    wanted = draw_wanted(jax.random.fold_in(jax.random.fold_in(keys[6], part), 71), part)
    return dict(source_emb=source_emb, target_emb=target_emb, tile_source=tile_source, tile_slot=tile_slot, tile_count=tile_count, wanted=wanted)


EPSILON = 1e-06
SOFTMAX_WARMTH = 0.03
ROW_MINIMUM = 1.0
COLUMN_FLOOR = 0.01
HIGHEST = lax.Precision.HIGHEST

def unit_rows(values):
    return values * lax.rsqrt(lax.optimization_barrier(jnp.sum(values * values, axis=-1, keepdims=True)) + EPSILON)

def tile_kernel(source_tiles, target_tiles):
    cosine_affinity = jnp.einsum('tie,tje->tij', source_tiles, target_tiles, precision=HIGHEST)
    return jnp.exp(cosine_affinity / SOFTMAX_WARMTH)

def reference(source_emb, target_emb, tile_source, tile_slot, tile_count, wanted):
    source_normalized = unit_rows(source_emb).reshape(N_ROWS, SB_DEV, BLOCK, E)
    target_unit = unit_rows(target_emb).reshape(N_ROWS * TB_DEV, BLOCK, E)
    sources = tile_source.reshape(N_ROWS, CAP).astype(jnp.int32)
    slots = tile_slot.reshape(N_ROWS, CAP).astype(jnp.int32)
    requests = wanted.reshape(N_ROWS, N_ROWS * NEED).astype(jnp.int32)
    local_blocks = jnp.take_along_axis(requests, slots, axis=1)
    global_ids = (slots // NEED * TB_DEV + local_blocks).astype(jnp.int32)
    live = (jnp.arange(CAP)[None, :] < tile_count[:, None]).astype(jnp.float32)
    block_range = jnp.arange(SB_DEV).astype(jnp.int32)
    target_range = jnp.arange(N_ROWS * TB_DEV).astype(jnp.int32)
    device_inputs = (source_normalized, sources, global_ids, live)

    def affinity_tiles(device_source, source_ids, target_ids, live_slots):
        return tile_kernel(device_source[source_ids], target_unit[target_ids]) * live_slots[:, None, None]

    def row_scale_of(column_scale):

        def per_device(inputs):
            device_source, source_ids, target_ids, live_slots = inputs
            tiles = affinity_tiles(device_source, source_ids, target_ids, live_slots)
            partials = jnp.einsum('tij,tj->ti', tiles, column_scale[target_ids], precision=HIGHEST)
            onehot = (source_ids[:, None] == block_range[None, :]).astype(jnp.float32)
            row_sums = jnp.einsum('ts,ti->si', onehot, partials, precision=HIGHEST)
            return 1.0 / jnp.maximum(row_sums, ROW_MINIMUM)
        return lax.map(per_device, device_inputs)

    def column_scale_of(row_scale):

        def per_device(inputs):
            device_source, source_ids, target_ids, live_slots, device_rows = inputs
            tiles = affinity_tiles(device_source, source_ids, target_ids, live_slots)
            partials = jnp.einsum('tij,ti->tj', tiles, device_rows[source_ids], precision=HIGHEST)
            onehot = (target_ids[:, None] == target_range[None, :]).astype(jnp.float32)
            return jnp.einsum('tn,tj->nj', onehot, partials, precision=HIGHEST)
        column_partials = lax.map(per_device, device_inputs + (row_scale,))
        return 1.0 / jnp.maximum(lax.optimization_barrier(jnp.sum(column_partials, axis=0)), COLUMN_FLOOR)
    column_scale = jnp.ones((N_ROWS * TB_DEV, BLOCK), jnp.float32)
    row_scale = jnp.ones((N_ROWS, SB_DEV, BLOCK), jnp.float32)
    for iteration in range(ITERS):
        row_scale = row_scale_of(column_scale)
        column_scale = column_scale_of(row_scale)

    def final_device(inputs):
        device_source, source_ids, target_ids, live_slots, device_rows = inputs
        tiles = affinity_tiles(device_source, source_ids, target_ids, live_slots)
        weights = tiles * device_rows[source_ids][:, :, None] * column_scale[target_ids][:, None, :]
        onehot = (source_ids[:, None] == block_range[None, :]).astype(jnp.float32)
        vectors = jnp.einsum('tij,tje->tie', weights, target_unit[target_ids], precision=HIGHEST)
        aligned_rows = jnp.einsum('ts,tie->sie', onehot, vectors, precision=HIGHEST)
        mass_rows = jnp.einsum('ts,ti->si', onehot, lax.optimization_barrier(jnp.sum(weights, axis=2)), precision=HIGHEST)
        return (aligned_rows, mass_rows)
    aligned_all, mass_all = lax.map(final_device, device_inputs + (row_scale,))
    aligned = (aligned_all * math.sqrt(E)).reshape(N_ROWS * SB_DEV * BLOCK, E)
    return (aligned, mass_all.reshape(N_ROWS * SB_DEV * BLOCK))
```

```python
import math

import jax
import jax.numpy as jnp
from jax import lax
from jax.experimental import pallas as pl
from jax.experimental.pallas import tpu as pltpu
from jax.sharding import PartitionSpec as P

E = 128
BLOCK = 128
ITERS = 2
SUB = 8

EPSILON = 1e-06
SOFTMAX_WARMTH = 0.03
ROW_MINIMUM = 1.0
COLUMN_FLOOR = 0.01
HIGHEST = lax.Precision.HIGHEST

NT = (((1,), (1,)), ((), ()))


def unit_rows(values):
    return values * lax.rsqrt(jnp.sum(values * values, axis=-1, keepdims=True) + EPSILON)


def _tile(s_ref, t_ref, q, o):
    cosine = lax.dot_general(
        s_ref[q], t_ref[o], NT, precision=HIGHEST, preferred_element_type=jnp.float32
    )
    return jnp.exp(cosine / SOFTMAX_WARMTH)


def _sweep_kernel(src_sm, slot_sm, cnt_sm, s_ref, t_ref, c_ref, r_out, colp_out, k_scr, rs_scr):
    live = cnt_sm[0]
    rs_scr[...] = jnp.zeros_like(rs_scr)
    colp_out[...] = jnp.zeros_like(colp_out)

    def rows(t, carry):
        q = src_sm[t]
        o = slot_sm[t]
        k = _tile(s_ref, t_ref, q, o)
        k_scr[t] = k
        rs_scr[q] += lax.dot_general(
            c_ref[o], k, NT, precision=HIGHEST, preferred_element_type=jnp.float32
        )
        return carry

    lax.fori_loop(0, live, rows, 0)
    r_out[...] = 1.0 / jnp.maximum(rs_scr[...], ROW_MINIMUM)

    def cols(t, carry):
        q = src_sm[t]
        o = slot_sm[t]
        colp_out[o] += jnp.dot(
            r_out[q], k_scr[t], precision=HIGHEST, preferred_element_type=jnp.float32
        )
        return carry

    lax.fori_loop(0, live, cols, 0)


def _final_kernel(src_sm, slot_sm, cnt_sm, s_ref, t_ref, c_ref, al_out, ms_out):
    live = cnt_sm[0]
    al_out[...] = jnp.zeros_like(al_out)
    ms_out[...] = jnp.zeros_like(ms_out)
    ones = jnp.ones((SUB, BLOCK), jnp.float32)

    def body(t, carry):
        q = src_sm[t]
        o = slot_sm[t]
        k = _tile(s_ref, t_ref, q, o)
        kc = k * c_ref[o][0:1, :]
        al_out[q] += jnp.dot(kc, t_ref[o], precision=HIGHEST, preferred_element_type=jnp.float32)
        ms_out[q] += lax.dot_general(
            ones, kc, NT, precision=HIGHEST, preferred_element_type=jnp.float32
        )
        return carry

    lax.fori_loop(0, live, body, 0)


def _specs(n_smem, n_vmem):
    return [pl.BlockSpec(memory_space=pltpu.SMEM)] * n_smem + [
        pl.BlockSpec(memory_space=pltpu.VMEM)
    ] * n_vmem


def sweep(tile_source, tile_slot, tile_count, source_unit, fetched, col8):
    capacity = tile_source.shape[0]
    sb = source_unit.shape[0]
    slots = fetched.shape[0]
    return pl.pallas_call(
        _sweep_kernel,
        out_shape=(
            jax.ShapeDtypeStruct((sb, SUB, BLOCK), jnp.float32),
            jax.ShapeDtypeStruct((slots, SUB, BLOCK), jnp.float32),
        ),
        in_specs=_specs(3, 3),
        out_specs=(pl.BlockSpec(memory_space=pltpu.VMEM),) * 2,
        scratch_shapes=[
            pltpu.VMEM((capacity, BLOCK, BLOCK), jnp.float32),
            pltpu.VMEM((sb, SUB, BLOCK), jnp.float32),
        ],
    )(tile_source, tile_slot, tile_count, source_unit, fetched, col8)


def final(tile_source, tile_slot, tile_count, source_unit, fetched, col8):
    sb = source_unit.shape[0]
    return pl.pallas_call(
        _final_kernel,
        out_shape=(
            jax.ShapeDtypeStruct((sb, BLOCK, E), jnp.float32),
            jax.ShapeDtypeStruct((sb, SUB, BLOCK), jnp.float32),
        ),
        in_specs=_specs(3, 3),
        out_specs=(pl.BlockSpec(memory_space=pltpu.VMEM),) * 2,
    )(tile_source, tile_slot, tile_count, source_unit, fetched, col8)


def on_device(source_emb, target_emb, tile_source, tile_slot, tile_count, wanted):
    rows_n = lax.axis_size("rows")
    need = wanted.shape[1]
    target_blocks = target_emb.shape[0] // BLOCK
    slots = rows_n * need
    source_unit = unit_rows(source_emb).reshape(-1, BLOCK, E)
    asked = lax.all_to_all(wanted, "rows", split_axis=0, concat_axis=0, tiled=True)
    own_unit = unit_rows(target_emb).reshape(target_blocks, BLOCK, E)
    outgoing = own_unit[asked.reshape(-1)]
    fetched = lax.all_to_all(outgoing, "rows", split_axis=0, concat_axis=0, tiled=True)
    owner_match = asked.reshape(slots)[:, None] == jnp.arange(target_blocks)[None, :]

    def column_scale_of(colp8):
        partial = colp8[:, 0, :].reshape(rows_n, need * BLOCK)
        received = lax.all_to_all(partial, "rows", split_axis=0, concat_axis=0, tiled=True)
        received = received.reshape(slots, BLOCK)
        totals = jnp.sum(
            jnp.where(owner_match[:, :, None], received[:, None, :], 0.0), axis=0
        )
        scales = 1.0 / jnp.maximum(totals, COLUMN_FLOOR)
        back = jnp.take(scales, asked.reshape(slots), axis=0).reshape(rows_n, need * BLOCK)
        col = lax.all_to_all(back, "rows", split_axis=0, concat_axis=0, tiled=True)
        return jnp.broadcast_to(col.reshape(slots, 1, BLOCK), (slots, SUB, BLOCK))

    col8 = jnp.ones((slots, SUB, BLOCK), jnp.float32)
    row8 = None
    for iteration in range(ITERS):
        row8, colp8 = sweep(tile_source, tile_slot, tile_count, source_unit, fetched, col8)
        col8 = column_scale_of(colp8)
    al, ms = final(tile_source, tile_slot, tile_count, source_unit, fetched, col8)
    row_scale = row8[:, 0, :]
    aligned = (al * row_scale[:, :, None]) * math.sqrt(E)
    mass = ms[:, 0, :] * row_scale
    return (aligned.reshape(-1, E), mass.reshape(-1))


def solution(mesh):
    placed = (
        P(("groups", "rows"), None),
        P(("groups", "rows"), None),
        P(("groups", "rows")),
        P(("groups", "rows")),
        P(("groups", "rows")),
        P(("groups", "rows"), None),
    )
    return jax.shard_map(
        on_device,
        mesh=mesh,
        in_specs=placed,
        out_specs=(P(("groups", "rows"), None), P(("groups", "rows"))),
        check_vma=False,
    )
```

```python
import math

import jax
import jax.numpy as jnp
from jax import lax
from jax.experimental import pallas as pl
from jax.experimental.pallas import tpu as pltpu
from jax.sharding import PartitionSpec as P

E = 128
BLOCK = 128
ITERS = 2
UNROLL = 4

EPSILON = 1e-06
SOFTMAX_WARMTH = 0.03
ROW_MINIMUM = 1.0
COLUMN_FLOOR = 0.01
HIGHEST = lax.Precision.HIGHEST

NT = (((1,), (1,)), ((), ()))


def unit_rows(values):
    return values * lax.rsqrt(jnp.sum(values * values, axis=-1, keepdims=True) + EPSILON)


def _tile(s_ref, t_ref, q, o):
    cosine = lax.dot_general(
        s_ref[q], t_ref[o], NT, precision=HIGHEST, preferred_element_type=jnp.float32
    )
    return jnp.exp(cosine / SOFTMAX_WARMTH)


def _sweep_kernel(src_sm, slot_sm, live_ref, s_ref, t_ref, c_ref, r_out, colp_out, k_scr, rs_scr):
    capacity = k_scr.shape[0]
    rs_scr[...] = jnp.zeros_like(rs_scr)
    colp_out[...] = jnp.zeros_like(colp_out)

    def rows(t, carry):
        q = src_sm[t]
        o = slot_sm[t]
        k = _tile(s_ref, t_ref, q, o) * live_ref[t]
        k_scr[t] = k
        rs_scr[q] += jnp.sum(k * c_ref[o], axis=1, keepdims=True)
        return carry

    lax.fori_loop(0, capacity, rows, 0, unroll=UNROLL)
    r_out[...] = 1.0 / jnp.maximum(rs_scr[...], ROW_MINIMUM)

    def cols(t, carry):
        q = src_sm[t]
        o = slot_sm[t]
        colp_out[o] += jnp.sum(k_scr[t] * r_out[q], axis=0, keepdims=True)
        return carry

    lax.fori_loop(0, capacity, cols, 0, unroll=UNROLL)


def _final_kernel(src_sm, slot_sm, live_ref, s_ref, t_ref, c_ref, r_ref, al_out, ms_out):
    capacity = src_sm.shape[0]
    al_out[...] = jnp.zeros_like(al_out)
    ms_out[...] = jnp.zeros_like(ms_out)

    def body(t, carry):
        q = src_sm[t]
        o = slot_sm[t]
        kc = (_tile(s_ref, t_ref, q, o) * live_ref[t]) * c_ref[o]
        al_out[q] += jnp.dot(kc, t_ref[o], precision=HIGHEST, preferred_element_type=jnp.float32)
        ms_out[q] += jnp.sum(kc, axis=1, keepdims=True)
        return carry

    lax.fori_loop(0, capacity, body, 0, unroll=UNROLL)
    r = r_ref[...]
    al_out[...] = al_out[...] * r * math.sqrt(E)
    ms_out[...] = ms_out[...] * r


def _specs(n_smem, n_vmem):
    return [pl.BlockSpec(memory_space=pltpu.SMEM)] * n_smem + [
        pl.BlockSpec(memory_space=pltpu.VMEM)
    ] * n_vmem


def sweep(tile_source, tile_slot, live, source_unit, fetched, col):
    capacity = tile_source.shape[0]
    sb = source_unit.shape[0]
    slots = fetched.shape[0]
    return pl.pallas_call(
        _sweep_kernel,
        out_shape=(
            jax.ShapeDtypeStruct((sb, BLOCK, 1), jnp.float32),
            jax.ShapeDtypeStruct((slots, 1, BLOCK), jnp.float32),
        ),
        in_specs=_specs(3, 3),
        out_specs=(pl.BlockSpec(memory_space=pltpu.VMEM),) * 2,
        scratch_shapes=[
            pltpu.VMEM((capacity, BLOCK, BLOCK), jnp.float32),
            pltpu.VMEM((sb, BLOCK, 1), jnp.float32),
        ],
    )(tile_source, tile_slot, live, source_unit, fetched, col)


def final(tile_source, tile_slot, live, source_unit, fetched, col, row):
    sb = source_unit.shape[0]
    return pl.pallas_call(
        _final_kernel,
        out_shape=(
            jax.ShapeDtypeStruct((sb, BLOCK, E), jnp.float32),
            jax.ShapeDtypeStruct((sb, BLOCK, 1), jnp.float32),
        ),
        in_specs=_specs(3, 4),
        out_specs=(pl.BlockSpec(memory_space=pltpu.VMEM),) * 2,
    )(tile_source, tile_slot, live, source_unit, fetched, col, row)


def on_device(source_emb, target_emb, tile_source, tile_slot, tile_count, wanted):
    rows_n = lax.axis_size("rows")
    need = wanted.shape[1]
    target_blocks = target_emb.shape[0] // BLOCK
    slots = rows_n * need
    source_unit = unit_rows(source_emb).reshape(-1, BLOCK, E)
    asked = lax.all_to_all(wanted, "rows", split_axis=0, concat_axis=0, tiled=True)
    own_unit = unit_rows(target_emb).reshape(target_blocks, BLOCK, E)
    outgoing = own_unit[asked.reshape(-1)]
    fetched = lax.all_to_all(outgoing, "rows", split_axis=0, concat_axis=0, tiled=True)
    owner_match = asked.reshape(slots)[:, None] == jnp.arange(target_blocks)[None, :]

    def column_scale_of(colp):
        partial = colp.reshape(rows_n, need * BLOCK)
        received = lax.all_to_all(partial, "rows", split_axis=0, concat_axis=0, tiled=True)
        received = received.reshape(slots, BLOCK)
        totals = jnp.sum(
            jnp.where(owner_match[:, :, None], received[:, None, :], 0.0), axis=0
        )
        scales = 1.0 / jnp.maximum(totals, COLUMN_FLOOR)
        back = jnp.take(scales, asked.reshape(slots), axis=0).reshape(rows_n, need * BLOCK)
        col = lax.all_to_all(back, "rows", split_axis=0, concat_axis=0, tiled=True)
        return col.reshape(slots, 1, BLOCK)

    live = (jnp.arange(tile_source.shape[0]) < tile_count[0]).astype(jnp.float32)
    col = jnp.ones((slots, 1, BLOCK), jnp.float32)
    row = None
    for iteration in range(ITERS):
        row, colp = sweep(tile_source, tile_slot, live, source_unit, fetched, col)
        col = column_scale_of(colp)
    al, ms = final(tile_source, tile_slot, live, source_unit, fetched, col, row)
    return (al.reshape(-1, E), ms.reshape(-1))


def solution(mesh):
    placed = (
        P(("groups", "rows"), None),
        P(("groups", "rows"), None),
        P(("groups", "rows")),
        P(("groups", "rows")),
        P(("groups", "rows")),
        P(("groups", "rows"), None),
    )
    return jax.shard_map(
        on_device,
        mesh=mesh,
        in_specs=placed,
        out_specs=(P(("groups", "rows"), None), P(("groups", "rows"))),
        check_vma=False,
    )
```

```python
import math

import jax
import jax.numpy as jnp
from jax import lax
from jax.experimental import pallas as pl
from jax.experimental.pallas import tpu as pltpu
from jax.sharding import PartitionSpec as P

E = 128
BLOCK = 128
ITERS = 2
UNROLL = 4

EPSILON = 1e-06
SOFTMAX_WARMTH = 0.03
ROW_MINIMUM = 1.0
COLUMN_FLOOR = 0.01
HIGHEST = lax.Precision.HIGHEST

NT = (((1,), (1,)), ((), ()))


def unit_rows(values):
    return values * lax.rsqrt(jnp.sum(values * values, axis=-1, keepdims=True) + EPSILON)


def _tile(s_ref, t_ref, q, o):
    cosine = lax.dot_general(
        s_ref[q], t_ref[o], NT, precision=HIGHEST, preferred_element_type=jnp.float32
    )
    return jnp.exp(cosine / SOFTMAX_WARMTH)


def _rows_cols(src_sm, slot_sm, tile_at, k_ref, c_ref, r_out, colp_out, rs_scr):
    capacity = src_sm.shape[0]
    rs_scr[...] = jnp.zeros_like(rs_scr)
    colp_out[...] = jnp.zeros_like(colp_out)

    def rows(t, carry):
        q = src_sm[t]
        o = slot_sm[t]
        k = tile_at(t, q, o)
        rs_scr[q] += jnp.sum(k * c_ref[o], axis=1, keepdims=True)
        return carry

    lax.fori_loop(0, capacity, rows, 0, unroll=UNROLL)
    r_out[...] = 1.0 / jnp.maximum(rs_scr[...], ROW_MINIMUM)

    def cols(t, carry):
        q = src_sm[t]
        o = slot_sm[t]
        colp_out[o] += jnp.sum(k_ref[t] * r_out[q], axis=0, keepdims=True)
        return carry

    lax.fori_loop(0, capacity, cols, 0, unroll=UNROLL)


def _first_kernel(src_sm, slot_sm, live_ref, s_ref, t_ref, c_ref, k_out, r_out, colp_out, rs_scr):
    def build(t, q, o):
        k = _tile(s_ref, t_ref, q, o) * live_ref[t]
        k_out[t] = k
        return k

    _rows_cols(src_sm, slot_sm, build, k_out, c_ref, r_out, colp_out, rs_scr)


def _again_kernel(src_sm, slot_sm, k_ref, c_ref, r_out, colp_out, rs_scr):
    _rows_cols(src_sm, slot_sm, lambda t, q, o: k_ref[t], k_ref, c_ref, r_out, colp_out, rs_scr)


def _final_kernel(src_sm, slot_sm, k_ref, t_ref, c_ref, r_ref, al_out, ms_out):
    capacity = src_sm.shape[0]
    al_out[...] = jnp.zeros_like(al_out)
    ms_out[...] = jnp.zeros_like(ms_out)

    def body(t, carry):
        q = src_sm[t]
        o = slot_sm[t]
        kc = k_ref[t] * c_ref[o]
        al_out[q] += jnp.dot(kc, t_ref[o], precision=HIGHEST, preferred_element_type=jnp.float32)
        ms_out[q] += jnp.sum(kc, axis=1, keepdims=True)
        return carry

    lax.fori_loop(0, capacity, body, 0, unroll=UNROLL)
    r = r_ref[...]
    al_out[...] = al_out[...] * r * math.sqrt(E)
    ms_out[...] = ms_out[...] * r


def _specs(n_smem, n_vmem):
    return [pl.BlockSpec(memory_space=pltpu.SMEM)] * n_smem + [
        pl.BlockSpec(memory_space=pltpu.VMEM)
    ] * n_vmem


def _vmem_out(n):
    return (pl.BlockSpec(memory_space=pltpu.VMEM),) * n


def first_sweep(tile_source, tile_slot, live, source_unit, fetched, col):
    capacity = tile_source.shape[0]
    sb = source_unit.shape[0]
    slots = fetched.shape[0]
    return pl.pallas_call(
        _first_kernel,
        out_shape=(
            jax.ShapeDtypeStruct((capacity, BLOCK, BLOCK), jnp.float32),
            jax.ShapeDtypeStruct((sb, BLOCK, 1), jnp.float32),
            jax.ShapeDtypeStruct((slots, 1, BLOCK), jnp.float32),
        ),
        in_specs=_specs(3, 3),
        out_specs=_vmem_out(3),
        scratch_shapes=[pltpu.VMEM((sb, BLOCK, 1), jnp.float32)],
    )(tile_source, tile_slot, live, source_unit, fetched, col)


def again_sweep(tile_source, tile_slot, kernel, col, sb):
    slots = col.shape[0]
    return pl.pallas_call(
        _again_kernel,
        out_shape=(
            jax.ShapeDtypeStruct((sb, BLOCK, 1), jnp.float32),
            jax.ShapeDtypeStruct((slots, 1, BLOCK), jnp.float32),
        ),
        in_specs=_specs(2, 2),
        out_specs=_vmem_out(2),
        scratch_shapes=[pltpu.VMEM((sb, BLOCK, 1), jnp.float32)],
    )(tile_source, tile_slot, kernel, col)


def final(tile_source, tile_slot, kernel, fetched, col, row):
    sb = row.shape[0]
    return pl.pallas_call(
        _final_kernel,
        out_shape=(
            jax.ShapeDtypeStruct((sb, BLOCK, E), jnp.float32),
            jax.ShapeDtypeStruct((sb, BLOCK, 1), jnp.float32),
        ),
        in_specs=_specs(2, 4),
        out_specs=_vmem_out(2),
    )(tile_source, tile_slot, kernel, fetched, col, row)


def on_device(source_emb, target_emb, tile_source, tile_slot, tile_count, wanted):
    rows_n = lax.axis_size("rows")
    need = wanted.shape[1]
    target_blocks = target_emb.shape[0] // BLOCK
    slots = rows_n * need
    source_unit = unit_rows(source_emb).reshape(-1, BLOCK, E)
    asked = lax.all_to_all(wanted, "rows", split_axis=0, concat_axis=0, tiled=True)
    own_unit = unit_rows(target_emb).reshape(target_blocks, BLOCK, E)
    outgoing = own_unit[asked.reshape(-1)]
    fetched = lax.all_to_all(outgoing, "rows", split_axis=0, concat_axis=0, tiled=True)
    owner_match = asked.reshape(slots)[:, None] == jnp.arange(target_blocks)[None, :]

    def column_scale_of(colp):
        partial = colp.reshape(rows_n, need * BLOCK)
        received = lax.all_to_all(partial, "rows", split_axis=0, concat_axis=0, tiled=True)
        received = received.reshape(slots, BLOCK)
        totals = jnp.sum(
            jnp.where(owner_match[:, :, None], received[:, None, :], 0.0), axis=0
        )
        scales = 1.0 / jnp.maximum(totals, COLUMN_FLOOR)
        back = jnp.take(scales, asked.reshape(slots), axis=0).reshape(rows_n, need * BLOCK)
        col = lax.all_to_all(back, "rows", split_axis=0, concat_axis=0, tiled=True)
        return col.reshape(slots, 1, BLOCK)

    live = (jnp.arange(tile_source.shape[0]) < tile_count[0]).astype(jnp.float32)
    col = jnp.ones((slots, 1, BLOCK), jnp.float32)
    sb = source_unit.shape[0]
    kernel, row, colp = first_sweep(tile_source, tile_slot, live, source_unit, fetched, col)
    for iteration in range(1, ITERS):
        col = column_scale_of(colp)
        row, colp = again_sweep(tile_source, tile_slot, kernel, col, sb)
    col = column_scale_of(colp)
    al, ms = final(tile_source, tile_slot, kernel, fetched, col, row)
    return (al.reshape(-1, E), ms.reshape(-1))


def solution(mesh):
    placed = (
        P(("groups", "rows"), None),
        P(("groups", "rows"), None),
        P(("groups", "rows")),
        P(("groups", "rows")),
        P(("groups", "rows")),
        P(("groups", "rows"), None),
    )
    return jax.shard_map(
        on_device,
        mesh=mesh,
        in_specs=placed,
        out_specs=(P(("groups", "rows"), None), P(("groups", "rows"))),
        check_vma=False,
    )
```

```python
import math

import jax
import jax.numpy as jnp
from jax import lax
from jax.experimental import pallas as pl
from jax.experimental.pallas import tpu as pltpu
from jax.sharding import PartitionSpec as P

E = 128
BLOCK = 128
ITERS = 2
UNROLL = 4

EPSILON = 1e-06
SOFTMAX_WARMTH = 0.03
ROW_MINIMUM = 1.0
COLUMN_FLOOR = 0.01
HIGHEST = lax.Precision.HIGHEST

def unit_rows(values):
    return values * lax.rsqrt(jnp.sum(values * values, axis=-1, keepdims=True) + EPSILON)


def _tile(s_ref, tt_ref, q, o):
    cosine = jnp.dot(s_ref[q], tt_ref[o], precision=HIGHEST, preferred_element_type=jnp.float32)
    return jnp.exp(cosine / SOFTMAX_WARMTH)


def _rows_cols(src_sm, slot_sm, tile_at, k_ref, c_ref, r_out, colp_out, rs_scr):
    capacity = src_sm.shape[0]
    rs_scr[...] = jnp.zeros_like(rs_scr)
    colp_out[...] = jnp.zeros_like(colp_out)

    def rows(t, carry):
        q = src_sm[t]
        o = slot_sm[t]
        k = tile_at(t, q, o)
        rs_scr[q] += jnp.sum(k * c_ref[o], axis=1, keepdims=True)
        return carry

    lax.fori_loop(0, capacity, rows, 0, unroll=UNROLL)
    r_out[...] = 1.0 / jnp.maximum(rs_scr[...], ROW_MINIMUM)

    def cols(t, carry):
        q = src_sm[t]
        o = slot_sm[t]
        colp_out[o] += jnp.sum(k_ref[t] * r_out[q], axis=0, keepdims=True)
        return carry

    lax.fori_loop(0, capacity, cols, 0, unroll=UNROLL)


def _first_kernel(src_sm, slot_sm, live_ref, s_ref, t_ref, c_ref, k_out, r_out, colp_out, rs_scr):
    def build(t, q, o):
        k = _tile(s_ref, t_ref, q, o) * live_ref[t]
        k_out[t] = k
        return k

    _rows_cols(src_sm, slot_sm, build, k_out, c_ref, r_out, colp_out, rs_scr)


def _again_kernel(src_sm, slot_sm, k_ref, c_ref, r_out, colp_out, rs_scr):
    _rows_cols(src_sm, slot_sm, lambda t, q, o: k_ref[t], k_ref, c_ref, r_out, colp_out, rs_scr)


def _final_kernel(src_sm, slot_sm, k_ref, t_ref, c_ref, r_ref, al_out, ms_out, ms_scr):
    capacity = src_sm.shape[0]
    al_out[...] = jnp.zeros_like(al_out)
    ms_scr[...] = jnp.zeros_like(ms_scr)

    def body(t, carry):
        q = src_sm[t]
        o = slot_sm[t]
        kc = k_ref[t] * c_ref[o]
        al_out[q] += jnp.dot(kc, t_ref[o], precision=HIGHEST, preferred_element_type=jnp.float32)
        ms_scr[q] += jnp.sum(kc, axis=1, keepdims=True)
        return carry

    lax.fori_loop(0, capacity, body, 0, unroll=UNROLL)
    r = r_ref[...]
    al_out[...] = al_out[...] * r * math.sqrt(E)
    for q in range(ms_out.shape[0]):
        mass = jnp.broadcast_to(ms_scr[q] * r_ref[q], (BLOCK, BLOCK))
        ms_out[q : q + 1, :] = jnp.transpose(mass)[0:1, :]


def _specs(n_smem, n_vmem):
    return [pl.BlockSpec(memory_space=pltpu.SMEM)] * n_smem + [
        pl.BlockSpec(memory_space=pltpu.VMEM)
    ] * n_vmem


def _vmem_out(n):
    return (pl.BlockSpec(memory_space=pltpu.VMEM),) * n


def first_sweep(tile_source, tile_slot, live, source_unit, fetched, col):
    capacity = tile_source.shape[0]
    sb = source_unit.shape[0]
    slots = fetched.shape[0]
    return pl.pallas_call(
        _first_kernel,
        out_shape=(
            jax.ShapeDtypeStruct((capacity, BLOCK, BLOCK), jnp.float32),
            jax.ShapeDtypeStruct((sb, BLOCK, 1), jnp.float32),
            jax.ShapeDtypeStruct((slots, 1, BLOCK), jnp.float32),
        ),
        in_specs=_specs(3, 3),
        out_specs=_vmem_out(3),
        scratch_shapes=[pltpu.VMEM((sb, BLOCK, 1), jnp.float32)],
    )(tile_source, tile_slot, live, source_unit, fetched, col)


def again_sweep(tile_source, tile_slot, kernel, col, sb):
    slots = col.shape[0]
    return pl.pallas_call(
        _again_kernel,
        out_shape=(
            jax.ShapeDtypeStruct((sb, BLOCK, 1), jnp.float32),
            jax.ShapeDtypeStruct((slots, 1, BLOCK), jnp.float32),
        ),
        in_specs=_specs(2, 2),
        out_specs=_vmem_out(2),
        scratch_shapes=[pltpu.VMEM((sb, BLOCK, 1), jnp.float32)],
    )(tile_source, tile_slot, kernel, col)


def final(tile_source, tile_slot, kernel, fetched, col, row):
    sb = row.shape[0]
    return pl.pallas_call(
        _final_kernel,
        out_shape=(
            jax.ShapeDtypeStruct((sb, BLOCK, E), jnp.float32),
            jax.ShapeDtypeStruct((sb, BLOCK), jnp.float32),
        ),
        in_specs=_specs(2, 4),
        out_specs=_vmem_out(2),
        scratch_shapes=[pltpu.VMEM((sb, BLOCK, 1), jnp.float32)],
    )(tile_source, tile_slot, kernel, fetched, col, row)


def on_device(source_emb, target_emb, tile_source, tile_slot, tile_count, wanted):
    rows_n = lax.axis_size("rows")
    need = wanted.shape[1]
    target_blocks = target_emb.shape[0] // BLOCK
    slots = rows_n * need
    source_unit = unit_rows(source_emb).reshape(-1, BLOCK, E)
    asked = lax.all_to_all(wanted, "rows", split_axis=0, concat_axis=0, tiled=True)
    own_unit = unit_rows(target_emb).reshape(target_blocks, BLOCK, E)
    outgoing = own_unit[asked.reshape(-1)]
    fetched = lax.all_to_all(outgoing, "rows", split_axis=0, concat_axis=0, tiled=True)
    owner_match = asked.reshape(slots)[:, None] == jnp.arange(target_blocks)[None, :]

    def column_scale_of(colp):
        partial = colp.reshape(rows_n, need * BLOCK)
        received = lax.all_to_all(partial, "rows", split_axis=0, concat_axis=0, tiled=True)
        received = received.reshape(slots, BLOCK)
        totals = jnp.sum(
            jnp.where(owner_match[:, :, None], received[:, None, :], 0.0), axis=0
        )
        scales = 1.0 / jnp.maximum(totals, COLUMN_FLOOR)
        back = jnp.take(scales, asked.reshape(slots), axis=0).reshape(rows_n, need * BLOCK)
        col = lax.all_to_all(back, "rows", split_axis=0, concat_axis=0, tiled=True)
        return col.reshape(slots, 1, BLOCK)

    live = (jnp.arange(tile_source.shape[0]) < tile_count[0]).astype(jnp.float32)
    col = jnp.ones((slots, 1, BLOCK), jnp.float32)
    sb = source_unit.shape[0]
    fetched_t = jnp.swapaxes(fetched, 1, 2)
    kernel, row, colp = first_sweep(tile_source, tile_slot, live, source_unit, fetched_t, col)
    for iteration in range(1, ITERS):
        col = column_scale_of(colp)
        row, colp = again_sweep(tile_source, tile_slot, kernel, col, sb)
    col = column_scale_of(colp)
    al, ms = final(tile_source, tile_slot, kernel, fetched, col, row)
    return (al.reshape(-1, E), ms.reshape(-1))


def solution(mesh):
    placed = (
        P(("groups", "rows"), None),
        P(("groups", "rows"), None),
        P(("groups", "rows")),
        P(("groups", "rows")),
        P(("groups", "rows")),
        P(("groups", "rows"), None),
    )
    return jax.shard_map(
        on_device,
        mesh=mesh,
        in_specs=placed,
        out_specs=(P(("groups", "rows"), None), P(("groups", "rows"))),
        check_vma=False,
    )
```

```python
import math

import jax
import jax.numpy as jnp
from jax import lax
from jax.experimental import pallas as pl
from jax.experimental.pallas import tpu as pltpu
from jax.sharding import PartitionSpec as P

E = 128
BLOCK = 128
ITERS = 2
UNROLL = 4

EPSILON = 1e-06
SOFTMAX_WARMTH = 0.03
ROW_MINIMUM = 1.0
COLUMN_FLOOR = 0.01
HIGHEST = lax.Precision.HIGHEST

def unit_rows(values):
    return values * lax.rsqrt(jnp.sum(values * values, axis=-1, keepdims=True) + EPSILON)


def _tile(s_ref, tt_ref, q, o):
    cosine = jnp.dot(s_ref[q], tt_ref[o], precision=HIGHEST, preferred_element_type=jnp.float32)
    return jnp.exp(cosine / SOFTMAX_WARMTH)


def _chunk(capacity):
    return math.gcd(capacity, 16)


def _rows_cols(src_sm, slot_sm, tile_at, chunk_done, k_ref, c_ref, r_out, colp_out, rs_scr):
    capacity = src_sm.shape[0]
    step = _chunk(capacity)
    rs_scr[...] = jnp.zeros_like(rs_scr)
    colp_out[...] = jnp.zeros_like(colp_out)

    def rows(t, carry):
        q = src_sm[t]
        o = slot_sm[t]
        k = tile_at(t, q, o)
        rs_scr[q] += jnp.sum(k * c_ref[o], axis=1, keepdims=True)
        return carry

    for part in range(capacity // step):
        chunk_done(part, "before")
        lax.fori_loop(part * step, (part + 1) * step, rows, 0, unroll=UNROLL)
        chunk_done(part, "after")
    r_out[...] = 1.0 / jnp.maximum(rs_scr[...], ROW_MINIMUM)

    def cols(t, carry):
        q = src_sm[t]
        o = slot_sm[t]
        colp_out[o] += jnp.sum(k_ref[t] * r_out[q], axis=0, keepdims=True)
        return carry

    lax.fori_loop(0, capacity, cols, 0, unroll=UNROLL)


def _chunk_copies(src, dst, sems, capacity):
    step = _chunk(capacity)
    return [
        pltpu.make_async_copy(
            src.at[pl.ds(part * step, step)], dst.at[pl.ds(part * step, step)], sems.at[part]
        )
        for part in range(capacity // step)
    ]


def _first_kernel(
    src_sm, slot_sm, live_ref, s_ref, tt_ref, c_ref, k_hbm, r_out, colp_out, k_scr, rs_scr, sems
):
    capacity = src_sm.shape[0]
    copies = _chunk_copies(k_scr, k_hbm, sems, capacity)

    def build(t, q, o):
        k = _tile(s_ref, tt_ref, q, o) * live_ref[t]
        k_scr[t] = k
        return k

    def chunk_done(part, when):
        if when == "after":
            copies[part].start()

    _rows_cols(src_sm, slot_sm, build, chunk_done, k_scr, c_ref, r_out, colp_out, rs_scr)
    for copy in copies:
        copy.wait()


def _again_kernel(src_sm, slot_sm, k_hbm, c_ref, r_out, colp_out, k_scr, rs_scr, sems):
    capacity = src_sm.shape[0]
    copies = _chunk_copies(k_hbm, k_scr, sems, capacity)
    for copy in copies:
        copy.start()

    def chunk_done(part, when):
        if when == "before":
            copies[part].wait()

    _rows_cols(
        src_sm, slot_sm, lambda t, q, o: k_scr[t], chunk_done, k_scr, c_ref, r_out, colp_out, rs_scr
    )


def _final_kernel(src_sm, slot_sm, k_hbm, t_ref, c_ref, r_ref, al_out, ms_out, k_scr, ms_scr, sems):
    capacity = src_sm.shape[0]
    step = _chunk(capacity)
    copies = _chunk_copies(k_hbm, k_scr, sems, capacity)
    for copy in copies:
        copy.start()
    al_out[...] = jnp.zeros_like(al_out)
    ms_scr[...] = jnp.zeros_like(ms_scr)

    def body(t, carry):
        q = src_sm[t]
        o = slot_sm[t]
        kc = k_scr[t] * c_ref[o]
        al_out[q] += jnp.dot(kc, t_ref[o], precision=HIGHEST, preferred_element_type=jnp.float32)
        ms_scr[q] += jnp.sum(kc, axis=1, keepdims=True)
        return carry

    for part in range(capacity // step):
        copies[part].wait()
        lax.fori_loop(part * step, (part + 1) * step, body, 0, unroll=UNROLL)
    r = r_ref[...]
    al_out[...] = al_out[...] * r * math.sqrt(E)
    for q in range(ms_out.shape[0]):
        mass = jnp.broadcast_to(ms_scr[q] * r_ref[q], (BLOCK, BLOCK))
        ms_out[q : q + 1, :] = jnp.transpose(mass)[0:1, :]


def _specs(n_smem, n_vmem):
    return [pl.BlockSpec(memory_space=pltpu.SMEM)] * n_smem + [
        pl.BlockSpec(memory_space=pltpu.VMEM)
    ] * n_vmem


def _vmem_out(n):
    return (pl.BlockSpec(memory_space=pltpu.VMEM),) * n


_ANY = pl.BlockSpec(memory_space=pl.ANY)


def first_sweep(tile_source, tile_slot, live, source_unit, fetched_t, col):
    capacity = tile_source.shape[0]
    sb = source_unit.shape[0]
    slots = fetched_t.shape[0]
    return pl.pallas_call(
        _first_kernel,
        out_shape=(
            jax.ShapeDtypeStruct((capacity, BLOCK, BLOCK), jnp.float32),
            jax.ShapeDtypeStruct((sb, BLOCK, 1), jnp.float32),
            jax.ShapeDtypeStruct((slots, 1, BLOCK), jnp.float32),
        ),
        in_specs=_specs(3, 3),
        out_specs=(_ANY,) + _vmem_out(2),
        scratch_shapes=[
            pltpu.VMEM((capacity, BLOCK, BLOCK), jnp.float32),
            pltpu.VMEM((sb, BLOCK, 1), jnp.float32),
            pltpu.SemaphoreType.DMA((capacity // _chunk(capacity),)),
        ],
    )(tile_source, tile_slot, live, source_unit, fetched_t, col)


def again_sweep(tile_source, tile_slot, kernel, col, sb):
    capacity = tile_source.shape[0]
    slots = col.shape[0]
    return pl.pallas_call(
        _again_kernel,
        out_shape=(
            jax.ShapeDtypeStruct((sb, BLOCK, 1), jnp.float32),
            jax.ShapeDtypeStruct((slots, 1, BLOCK), jnp.float32),
        ),
        in_specs=_specs(2, 0) + [_ANY] + _specs(0, 1),
        out_specs=_vmem_out(2),
        scratch_shapes=[
            pltpu.VMEM((capacity, BLOCK, BLOCK), jnp.float32),
            pltpu.VMEM((sb, BLOCK, 1), jnp.float32),
            pltpu.SemaphoreType.DMA((capacity // _chunk(capacity),)),
        ],
    )(tile_source, tile_slot, kernel, col)


def final(tile_source, tile_slot, kernel, fetched, col, row):
    capacity = tile_source.shape[0]
    sb = row.shape[0]
    return pl.pallas_call(
        _final_kernel,
        out_shape=(
            jax.ShapeDtypeStruct((sb, BLOCK, E), jnp.float32),
            jax.ShapeDtypeStruct((sb, BLOCK), jnp.float32),
        ),
        in_specs=_specs(2, 0) + [_ANY] + _specs(0, 3),
        out_specs=_vmem_out(2),
        scratch_shapes=[
            pltpu.VMEM((capacity, BLOCK, BLOCK), jnp.float32),
            pltpu.VMEM((sb, BLOCK, 1), jnp.float32),
            pltpu.SemaphoreType.DMA((capacity // _chunk(capacity),)),
        ],
    )(tile_source, tile_slot, kernel, fetched, col, row)


def on_device(source_emb, target_emb, tile_source, tile_slot, tile_count, wanted):
    rows_n = lax.axis_size("rows")
    need = wanted.shape[1]
    target_blocks = target_emb.shape[0] // BLOCK
    slots = rows_n * need
    source_unit = unit_rows(source_emb).reshape(-1, BLOCK, E)
    asked = lax.all_to_all(wanted, "rows", split_axis=0, concat_axis=0, tiled=True)
    own_unit = unit_rows(target_emb).reshape(target_blocks, BLOCK, E)
    outgoing = own_unit[asked.reshape(-1)]
    fetched = lax.all_to_all(outgoing, "rows", split_axis=0, concat_axis=0, tiled=True)
    owner_match = asked.reshape(slots)[:, None] == jnp.arange(target_blocks)[None, :]

    def column_scale_of(colp):
        partial = colp.reshape(rows_n, need * BLOCK)
        received = lax.all_to_all(partial, "rows", split_axis=0, concat_axis=0, tiled=True)
        received = received.reshape(slots, BLOCK)
        totals = jnp.sum(
            jnp.where(owner_match[:, :, None], received[:, None, :], 0.0), axis=0
        )
        scales = 1.0 / jnp.maximum(totals, COLUMN_FLOOR)
        back = jnp.take(scales, asked.reshape(slots), axis=0).reshape(rows_n, need * BLOCK)
        col = lax.all_to_all(back, "rows", split_axis=0, concat_axis=0, tiled=True)
        return col.reshape(slots, 1, BLOCK)

    live = (jnp.arange(tile_source.shape[0]) < tile_count[0]).astype(jnp.float32)
    col = jnp.ones((slots, 1, BLOCK), jnp.float32)
    sb = source_unit.shape[0]
    fetched_t = jnp.swapaxes(fetched, 1, 2)
    kernel, row, colp = first_sweep(tile_source, tile_slot, live, source_unit, fetched_t, col)
    for iteration in range(1, ITERS):
        col = column_scale_of(colp)
        row, colp = again_sweep(tile_source, tile_slot, kernel, col, sb)
    col = column_scale_of(colp)
    al, ms = final(tile_source, tile_slot, kernel, fetched, col, row)
    return (al.reshape(-1, E), ms.reshape(-1))


def solution(mesh):
    placed = (
        P(("groups", "rows"), None),
        P(("groups", "rows"), None),
        P(("groups", "rows")),
        P(("groups", "rows")),
        P(("groups", "rows")),
        P(("groups", "rows"), None),
    )
    return jax.shard_map(
        on_device,
        mesh=mesh,
        in_specs=placed,
        out_specs=(P(("groups", "rows"), None), P(("groups", "rows"))),
        check_vma=False,
    )
```

```python
import math

import jax
import jax.numpy as jnp
from jax import lax
from jax.experimental import pallas as pl
from jax.experimental.pallas import tpu as pltpu
from jax.sharding import PartitionSpec as P

E = 128
BLOCK = 128
ITERS = 2
UNROLL = 4

EPSILON = 1e-06
SOFTMAX_WARMTH = 0.03
ROW_MINIMUM = 1.0
COLUMN_FLOOR = 0.01
HIGHEST = lax.Precision.HIGHEST

def unit_rows(values):
    return values * lax.rsqrt(jnp.sum(values * values, axis=-1, keepdims=True) + EPSILON)


def _tile(s_ref, tt_ref, q, o):
    cosine = jnp.dot(s_ref[q], tt_ref[o], precision=HIGHEST, preferred_element_type=jnp.float32)
    return jnp.exp(cosine / SOFTMAX_WARMTH)


def _chunk(capacity):
    return math.gcd(capacity, 16)


def _rows_cols(src_sm, slot_sm, tile_at, chunk_done, k_ref, c_ref, r_out, colp_out, rs_scr):
    capacity = src_sm.shape[0]
    step = _chunk(capacity)
    rs_scr[...] = jnp.zeros_like(rs_scr)
    colp_out[...] = jnp.zeros_like(colp_out)

    def rows(t, carry):
        q = src_sm[t]
        o = slot_sm[t]
        k = tile_at(t, q, o)
        rs_scr[q] += jnp.sum(k * c_ref[o], axis=1, keepdims=True)
        return carry

    for part in range(capacity // step):
        chunk_done(part, "before")
        lax.fori_loop(part * step, (part + 1) * step, rows, 0, unroll=UNROLL)
        chunk_done(part, "after")
    r_out[...] = 1.0 / jnp.maximum(rs_scr[...], ROW_MINIMUM)

    def cols(t, carry):
        q = src_sm[t]
        o = slot_sm[t]
        colp_out[o] += jnp.sum(k_ref[t] * r_out[q], axis=0, keepdims=True)
        return carry

    lax.fori_loop(0, capacity, cols, 0, unroll=UNROLL)


def _chunk_copies(src, dst, sems, capacity):
    step = _chunk(capacity)
    return [
        pltpu.make_async_copy(
            src.at[pl.ds(part * step, step)], dst.at[pl.ds(part * step, step)], sems.at[part]
        )
        for part in range(capacity // step)
    ]


def _first_kernel(
    src_sm, slot_sm, live_ref, s_ref, tt_ref, c_ref, k_hbm, r_out, colp_out, k_scr, rs_scr, sems
):
    capacity = src_sm.shape[0]
    copies = _chunk_copies(k_scr, k_hbm, sems, capacity)

    def build(t, q, o):
        k = _tile(s_ref, tt_ref, q, o) * live_ref[t]
        k_scr[t] = k
        return k

    def chunk_done(part, when):
        if when == "after":
            copies[part].start()

    _rows_cols(src_sm, slot_sm, build, chunk_done, k_scr, c_ref, r_out, colp_out, rs_scr)
    for copy in copies:
        copy.wait()


def _again_kernel(src_sm, slot_sm, k_hbm, c_ref, r_out, colp_out, k_scr, rs_scr, sems):
    capacity = src_sm.shape[0]
    copies = _chunk_copies(k_hbm, k_scr, sems, capacity)
    for copy in copies:
        copy.start()

    def chunk_done(part, when):
        if when == "before":
            copies[part].wait()

    _rows_cols(
        src_sm, slot_sm, lambda t, q, o: k_scr[t], chunk_done, k_scr, c_ref, r_out, colp_out, rs_scr
    )


def _final_kernel(src_sm, slot_sm, k_hbm, t_ref, c_ref, r_ref, al_out, ms_out, k_scr, ms_scr, sems):
    capacity = src_sm.shape[0]
    step = _chunk(capacity)
    copies = _chunk_copies(k_hbm, k_scr, sems, capacity)
    for copy in copies:
        copy.start()
    al_out[...] = jnp.zeros_like(al_out)
    ms_scr[...] = jnp.zeros_like(ms_scr)

    def body(t, carry):
        q = src_sm[t]
        o = slot_sm[t]
        kc = k_scr[t] * c_ref[o]
        al_out[q] += jnp.dot(kc, t_ref[o], precision=HIGHEST, preferred_element_type=jnp.float32)
        ms_scr[q] += jnp.sum(kc, axis=1, keepdims=True)
        return carry

    for part in range(capacity // step):
        copies[part].wait()
        lax.fori_loop(part * step, (part + 1) * step, body, 0, unroll=UNROLL)
    r = r_ref[...]
    al_out[...] = al_out[...] * r * math.sqrt(E)
    for q in range(ms_out.shape[0]):
        mass = jnp.broadcast_to(ms_scr[q] * r_ref[q], (BLOCK, BLOCK))
        ms_out[q : q + 1, :] = jnp.transpose(mass)[0:1, :]


def _specs(n_smem, n_vmem):
    return [pl.BlockSpec(memory_space=pltpu.SMEM)] * n_smem + [
        pl.BlockSpec(memory_space=pltpu.VMEM)
    ] * n_vmem


def _vmem_out(n):
    return (pl.BlockSpec(memory_space=pltpu.VMEM),) * n


_ANY = pl.BlockSpec(memory_space=pl.ANY)


def first_sweep(tile_source, tile_slot, live, source_unit, fetched_t, col):
    capacity = tile_source.shape[0]
    sb = source_unit.shape[0]
    slots = fetched_t.shape[0]
    return pl.pallas_call(
        _first_kernel,
        out_shape=(
            jax.ShapeDtypeStruct((capacity, BLOCK, BLOCK), jnp.float32),
            jax.ShapeDtypeStruct((sb, BLOCK, 1), jnp.float32),
            jax.ShapeDtypeStruct((slots, 1, BLOCK), jnp.float32),
        ),
        in_specs=_specs(3, 3),
        out_specs=(_ANY,) + _vmem_out(2),
        scratch_shapes=[
            pltpu.VMEM((capacity, BLOCK, BLOCK), jnp.float32),
            pltpu.VMEM((sb, BLOCK, 1), jnp.float32),
            pltpu.SemaphoreType.DMA((capacity // _chunk(capacity),)),
        ],
    )(tile_source, tile_slot, live, source_unit, fetched_t, col)


def again_sweep(tile_source, tile_slot, kernel, col, sb):
    capacity = tile_source.shape[0]
    slots = col.shape[0]
    return pl.pallas_call(
        _again_kernel,
        out_shape=(
            jax.ShapeDtypeStruct((sb, BLOCK, 1), jnp.float32),
            jax.ShapeDtypeStruct((slots, 1, BLOCK), jnp.float32),
        ),
        in_specs=_specs(2, 0) + [_ANY] + _specs(0, 1),
        out_specs=_vmem_out(2),
        scratch_shapes=[
            pltpu.VMEM((capacity, BLOCK, BLOCK), jnp.float32),
            pltpu.VMEM((sb, BLOCK, 1), jnp.float32),
            pltpu.SemaphoreType.DMA((capacity // _chunk(capacity),)),
        ],
    )(tile_source, tile_slot, kernel, col)


def final(tile_source, tile_slot, kernel, fetched, col, row):
    capacity = tile_source.shape[0]
    sb = row.shape[0]
    return pl.pallas_call(
        _final_kernel,
        out_shape=(
            jax.ShapeDtypeStruct((sb, BLOCK, E), jnp.float32),
            jax.ShapeDtypeStruct((sb, BLOCK), jnp.float32),
        ),
        in_specs=_specs(2, 0) + [_ANY] + _specs(0, 3),
        out_specs=_vmem_out(2),
        scratch_shapes=[
            pltpu.VMEM((capacity, BLOCK, BLOCK), jnp.float32),
            pltpu.VMEM((sb, BLOCK, 1), jnp.float32),
            pltpu.SemaphoreType.DMA((capacity // _chunk(capacity),)),
        ],
    )(tile_source, tile_slot, kernel, fetched, col, row)


def on_device(source_emb, target_emb, tile_source, tile_slot, tile_count, wanted):
    rows_n = lax.axis_size("rows")
    need = wanted.shape[1]
    target_blocks = target_emb.shape[0] // BLOCK
    slots = rows_n * need
    source_unit = unit_rows(source_emb).reshape(-1, BLOCK, E)
    owners = rows_n
    wanted_row = wanted.reshape(1, slots)
    wanted_all = lax.all_to_all(
        jnp.broadcast_to(wanted_row, (rows_n, slots)), "rows", split_axis=0, concat_axis=0, tiled=True
    )
    me = lax.axis_index("rows")
    asked = lax.dynamic_slice_in_dim(wanted_all, me * need, need, axis=1)
    own_unit = unit_rows(target_emb).reshape(target_blocks, BLOCK, E)
    outgoing = own_unit[asked.reshape(-1)]
    fetched = lax.all_to_all(outgoing, "rows", split_axis=0, concat_axis=0, tiled=True)
    same_block = (
        wanted_all.reshape(rows_n, owners, need, 1) == wanted.reshape(1, owners, 1, need)
    )[..., None]

    def column_scale_of(colp):
        spread = jnp.broadcast_to(colp.reshape(1, slots, BLOCK), (rows_n, slots, BLOCK))
        gathered = lax.all_to_all(spread, "rows", split_axis=0, concat_axis=0, tiled=True)
        gathered = gathered.reshape(rows_n, owners, need, 1, BLOCK)
        totals = jnp.sum(jnp.where(same_block, gathered, 0.0), axis=(0, 2))
        return (1.0 / jnp.maximum(totals, COLUMN_FLOOR)).reshape(slots, 1, BLOCK)

    live = (jnp.arange(tile_source.shape[0]) < tile_count[0]).astype(jnp.float32)
    col = jnp.ones((slots, 1, BLOCK), jnp.float32)
    sb = source_unit.shape[0]
    fetched_t = jnp.swapaxes(fetched, 1, 2)
    kernel, row, colp = first_sweep(tile_source, tile_slot, live, source_unit, fetched_t, col)
    for iteration in range(1, ITERS):
        col = column_scale_of(colp)
        row, colp = again_sweep(tile_source, tile_slot, kernel, col, sb)
    col = column_scale_of(colp)
    al, ms = final(tile_source, tile_slot, kernel, fetched, col, row)
    return (al.reshape(-1, E), ms.reshape(-1))


def solution(mesh):
    placed = (
        P(("groups", "rows"), None),
        P(("groups", "rows"), None),
        P(("groups", "rows")),
        P(("groups", "rows")),
        P(("groups", "rows")),
        P(("groups", "rows"), None),
    )
    return jax.shard_map(
        on_device,
        mesh=mesh,
        in_specs=placed,
        out_specs=(P(("groups", "rows"), None), P(("groups", "rows"))),
        check_vma=False,
    )
```

```python
import math

import jax
import jax.numpy as jnp
from jax import lax
from jax.experimental import pallas as pl
from jax.experimental.pallas import tpu as pltpu
from jax.sharding import PartitionSpec as P

E = 128
BLOCK = 128
ITERS = 2
UNROLL = 4

EPSILON = 1e-06
SOFTMAX_WARMTH = 0.03
ROW_MINIMUM = 1.0
COLUMN_FLOOR = 0.01
HIGHEST = lax.Precision.HIGHEST

def unit_rows(values):
    return values * lax.rsqrt(jnp.sum(values * values, axis=-1, keepdims=True) + EPSILON)


def _tile(s_ref, tt_ref, q, o):
    cosine = jnp.dot(s_ref[q], tt_ref[o], precision=HIGHEST, preferred_element_type=jnp.float32)
    return jnp.exp(cosine / SOFTMAX_WARMTH)


def _chunk(capacity):
    return math.gcd(capacity, 16)


def _rows_cols(src_sm, slot_sm, tile_at, chunk_done, k_ref, c_ref, r_out, colp_out, acc, rb_scr):
    capacity = src_sm.shape[0]
    sb = acc.shape[0]
    step = _chunk(capacity)
    acc[...] = jnp.zeros_like(acc)
    colp_out[...] = jnp.zeros_like(colp_out)

    def rows(t, carry):
        q = src_sm[t]
        o = slot_sm[t]
        acc[q] += tile_at(t, q, o) * c_ref[o]
        return carry

    for part in range(capacity // step):
        chunk_done(part, "before")
        lax.fori_loop(part * step, (part + 1) * step, rows, 0, unroll=UNROLL)
        chunk_done(part, "after")
    for q in range(sb):
        r = 1.0 / jnp.maximum(jnp.sum(acc[q], axis=1, keepdims=True), ROW_MINIMUM)
        r_out[q] = r
        rb_scr[q] = jnp.broadcast_to(r, (BLOCK, BLOCK))

    def cols(t, carry):
        q = src_sm[t]
        o = slot_sm[t]
        colp_out[o] += jnp.sum(k_ref[t] * rb_scr[q], axis=0, keepdims=True)
        return carry

    lax.fori_loop(0, capacity, cols, 0, unroll=UNROLL)


def _chunk_copies(src, dst, sems, capacity):
    step = _chunk(capacity)
    return [
        pltpu.make_async_copy(
            src.at[pl.ds(part * step, step)], dst.at[pl.ds(part * step, step)], sems.at[part]
        )
        for part in range(capacity // step)
    ]


def _first_kernel(
    src_sm, slot_sm, live_ref, s_ref, tt_ref, c_ref, k_hbm, r_out, colp_out, k_scr, acc, rb_scr, sems
):
    capacity = src_sm.shape[0]
    copies = _chunk_copies(k_scr, k_hbm, sems, capacity)

    def build(t, q, o):
        k = _tile(s_ref, tt_ref, q, o) * live_ref[t]
        k_scr[t] = k
        return k

    def chunk_done(part, when):
        if when == "after":
            copies[part].start()

    _rows_cols(src_sm, slot_sm, build, chunk_done, k_scr, c_ref, r_out, colp_out, acc, rb_scr)
    for copy in copies:
        copy.wait()


def _again_kernel(src_sm, slot_sm, k_hbm, c_ref, r_out, colp_out, k_scr, acc, rb_scr, sems):
    capacity = src_sm.shape[0]
    copies = _chunk_copies(k_hbm, k_scr, sems, capacity)
    for copy in copies:
        copy.start()

    def chunk_done(part, when):
        if when == "before":
            copies[part].wait()

    _rows_cols(
        src_sm, slot_sm, lambda t, q, o: k_scr[t], chunk_done, k_scr, c_ref, r_out, colp_out, acc, rb_scr
    )


def _final_kernel(src_sm, slot_sm, k_hbm, t_ref, c_ref, r_ref, al_out, ms_out, k_scr, ms_scr, sems):
    capacity = src_sm.shape[0]
    step = _chunk(capacity)
    copies = _chunk_copies(k_hbm, k_scr, sems, capacity)
    for copy in copies:
        copy.start()
    al_out[...] = jnp.zeros_like(al_out)
    ms_scr[...] = jnp.zeros_like(ms_scr)

    def body(t, carry):
        q = src_sm[t]
        o = slot_sm[t]
        kc = k_scr[t] * c_ref[o]
        al_out[q] += jnp.dot(kc, t_ref[o], precision=HIGHEST, preferred_element_type=jnp.float32)
        ms_scr[q] += kc
        return carry

    for part in range(capacity // step):
        copies[part].wait()
        lax.fori_loop(part * step, (part + 1) * step, body, 0, unroll=UNROLL)
    r = r_ref[...]
    al_out[...] = al_out[...] * r * math.sqrt(E)
    for q in range(ms_out.shape[0]):
        mass = jnp.broadcast_to(jnp.sum(ms_scr[q], axis=1, keepdims=True) * r_ref[q], (BLOCK, BLOCK))
        ms_out[q : q + 1, :] = jnp.transpose(mass)[0:1, :]


def _specs(n_smem, n_vmem):
    return [pl.BlockSpec(memory_space=pltpu.SMEM)] * n_smem + [
        pl.BlockSpec(memory_space=pltpu.VMEM)
    ] * n_vmem


def _vmem_out(n):
    return (pl.BlockSpec(memory_space=pltpu.VMEM),) * n


_ANY = pl.BlockSpec(memory_space=pl.ANY)


def first_sweep(tile_source, tile_slot, live, source_unit, fetched_t, col):
    capacity = tile_source.shape[0]
    sb = source_unit.shape[0]
    slots = fetched_t.shape[0]
    return pl.pallas_call(
        _first_kernel,
        out_shape=(
            jax.ShapeDtypeStruct((capacity, BLOCK, BLOCK), jnp.float32),
            jax.ShapeDtypeStruct((sb, BLOCK, 1), jnp.float32),
            jax.ShapeDtypeStruct((slots, 1, BLOCK), jnp.float32),
        ),
        in_specs=_specs(3, 3),
        out_specs=(_ANY,) + _vmem_out(2),
        scratch_shapes=[
            pltpu.VMEM((capacity, BLOCK, BLOCK), jnp.float32),
            pltpu.VMEM((sb, BLOCK, BLOCK), jnp.float32),
            pltpu.VMEM((sb, BLOCK, BLOCK), jnp.float32),
            pltpu.SemaphoreType.DMA((capacity // _chunk(capacity),)),
        ],
    )(tile_source, tile_slot, live, source_unit, fetched_t, col)


def again_sweep(tile_source, tile_slot, kernel, col, sb):
    capacity = tile_source.shape[0]
    slots = col.shape[0]
    return pl.pallas_call(
        _again_kernel,
        out_shape=(
            jax.ShapeDtypeStruct((sb, BLOCK, 1), jnp.float32),
            jax.ShapeDtypeStruct((slots, 1, BLOCK), jnp.float32),
        ),
        in_specs=_specs(2, 0) + [_ANY] + _specs(0, 1),
        out_specs=_vmem_out(2),
        scratch_shapes=[
            pltpu.VMEM((capacity, BLOCK, BLOCK), jnp.float32),
            pltpu.VMEM((sb, BLOCK, BLOCK), jnp.float32),
            pltpu.VMEM((sb, BLOCK, BLOCK), jnp.float32),
            pltpu.SemaphoreType.DMA((capacity // _chunk(capacity),)),
        ],
    )(tile_source, tile_slot, kernel, col)


def final(tile_source, tile_slot, kernel, fetched, col, row):
    capacity = tile_source.shape[0]
    sb = row.shape[0]
    return pl.pallas_call(
        _final_kernel,
        out_shape=(
            jax.ShapeDtypeStruct((sb, BLOCK, E), jnp.float32),
            jax.ShapeDtypeStruct((sb, BLOCK), jnp.float32),
        ),
        in_specs=_specs(2, 0) + [_ANY] + _specs(0, 3),
        out_specs=_vmem_out(2),
        scratch_shapes=[
            pltpu.VMEM((capacity, BLOCK, BLOCK), jnp.float32),
            pltpu.VMEM((sb, BLOCK, BLOCK), jnp.float32),
            pltpu.SemaphoreType.DMA((capacity // _chunk(capacity),)),
        ],
    )(tile_source, tile_slot, kernel, fetched, col, row)


def on_device(source_emb, target_emb, tile_source, tile_slot, tile_count, wanted):
    rows_n = lax.axis_size("rows")
    need = wanted.shape[1]
    target_blocks = target_emb.shape[0] // BLOCK
    slots = rows_n * need
    source_unit = unit_rows(source_emb).reshape(-1, BLOCK, E)
    owners = rows_n
    wanted_row = wanted.reshape(1, slots)
    wanted_all = lax.all_to_all(
        jnp.broadcast_to(wanted_row, (rows_n, slots)), "rows", split_axis=0, concat_axis=0, tiled=True
    )
    me = lax.axis_index("rows")
    asked = lax.dynamic_slice_in_dim(wanted_all, me * need, need, axis=1)
    own_unit = unit_rows(target_emb).reshape(target_blocks, BLOCK, E)
    outgoing = own_unit[asked.reshape(-1)]
    fetched = lax.all_to_all(outgoing, "rows", split_axis=0, concat_axis=0, tiled=True)
    same_block = (
        wanted_all.reshape(rows_n, owners, need, 1) == wanted.reshape(1, owners, 1, need)
    )[..., None]

    def column_scale_of(colp):
        spread = jnp.broadcast_to(colp.reshape(1, slots, BLOCK), (rows_n, slots, BLOCK))
        gathered = lax.all_to_all(spread, "rows", split_axis=0, concat_axis=0, tiled=True)
        gathered = gathered.reshape(rows_n, owners, need, 1, BLOCK)
        totals = jnp.sum(jnp.where(same_block, gathered, 0.0), axis=(0, 2))
        return (1.0 / jnp.maximum(totals, COLUMN_FLOOR)).reshape(slots, 1, BLOCK)

    live = (jnp.arange(tile_source.shape[0]) < tile_count[0]).astype(jnp.float32)
    col = jnp.ones((slots, 1, BLOCK), jnp.float32)
    sb = source_unit.shape[0]
    fetched_t = jnp.swapaxes(fetched, 1, 2)
    kernel, row, colp = first_sweep(tile_source, tile_slot, live, source_unit, fetched_t, col)
    for iteration in range(1, ITERS):
        col = column_scale_of(colp)
        row, colp = again_sweep(tile_source, tile_slot, kernel, col, sb)
    col = column_scale_of(colp)
    al, ms = final(tile_source, tile_slot, kernel, fetched, col, row)
    return (al.reshape(-1, E), ms.reshape(-1))


def solution(mesh):
    placed = (
        P(("groups", "rows"), None),
        P(("groups", "rows"), None),
        P(("groups", "rows")),
        P(("groups", "rows")),
        P(("groups", "rows")),
        P(("groups", "rows"), None),
    )
    return jax.shard_map(
        on_device,
        mesh=mesh,
        in_specs=placed,
        out_specs=(P(("groups", "rows"), None), P(("groups", "rows"))),
        check_vma=False,
    )
```

```python
import math

import jax
import jax.numpy as jnp
from jax import lax
from jax.experimental import pallas as pl
from jax.experimental.pallas import tpu as pltpu
from jax.sharding import PartitionSpec as P

E = 128
BLOCK = 128
ITERS = 2
UNROLL = 4

EPSILON = 1e-06
SOFTMAX_WARMTH = 0.03
ROW_MINIMUM = 1.0
COLUMN_FLOOR = 0.01
HIGHEST = lax.Precision.HIGHEST
HIGH = lax.Precision.HIGH

def unit_rows(values):
    return values * lax.rsqrt(jnp.sum(values * values, axis=-1, keepdims=True) + EPSILON)


def _tile(s_ref, tt_ref, q, o):
    cosine = jnp.dot(s_ref[q], tt_ref[o], precision=HIGHEST, preferred_element_type=jnp.float32)
    return jnp.exp(cosine / SOFTMAX_WARMTH)


def _chunk(capacity):
    return math.gcd(capacity, 16)


def _rows_cols(src_sm, slot_sm, tile_at, chunk_done, k_ref, c_ref, r_out, colp_out, acc, rb_scr):
    capacity = src_sm.shape[0]
    sb = acc.shape[0]
    step = _chunk(capacity)
    acc[...] = jnp.zeros_like(acc)
    colp_out[...] = jnp.zeros_like(colp_out)

    def rows(t, carry):
        q = src_sm[t]
        o = slot_sm[t]
        acc[q] += tile_at(t, q, o) * c_ref[o]
        return carry

    for part in range(capacity // step):
        chunk_done(part, "before")
        lax.fori_loop(part * step, (part + 1) * step, rows, 0, unroll=UNROLL)
        chunk_done(part, "after")
    for q in range(sb):
        r = 1.0 / jnp.maximum(jnp.sum(acc[q], axis=1, keepdims=True), ROW_MINIMUM)
        r_out[q] = r
        rb_scr[q] = jnp.broadcast_to(r, (BLOCK, BLOCK))

    def cols(t, carry):
        q = src_sm[t]
        o = slot_sm[t]
        colp_out[o] += jnp.sum(k_ref[t] * rb_scr[q], axis=0, keepdims=True)
        return carry

    lax.fori_loop(0, capacity, cols, 0, unroll=UNROLL)


def _chunk_copies(src, dst, sems, capacity):
    step = _chunk(capacity)
    return [
        pltpu.make_async_copy(
            src.at[pl.ds(part * step, step)], dst.at[pl.ds(part * step, step)], sems.at[part]
        )
        for part in range(capacity // step)
    ]


def _first_kernel(
    src_sm, slot_sm, live_ref, s_ref, tt_ref, c_ref, k_hbm, r_out, colp_out, k_scr, acc, rb_scr, sems
):
    capacity = src_sm.shape[0]
    copies = _chunk_copies(k_scr, k_hbm, sems, capacity)

    def build(t, q, o):
        k = _tile(s_ref, tt_ref, q, o) * live_ref[t]
        k_scr[t] = k
        return k

    def chunk_done(part, when):
        if when == "after":
            copies[part].start()

    _rows_cols(src_sm, slot_sm, build, chunk_done, k_scr, c_ref, r_out, colp_out, acc, rb_scr)
    for copy in copies:
        copy.wait()


def _again_kernel(src_sm, slot_sm, k_hbm, c_ref, r_out, colp_out, k_scr, acc, rb_scr, sems):
    capacity = src_sm.shape[0]
    copies = _chunk_copies(k_hbm, k_scr, sems, capacity)
    for copy in copies:
        copy.start()

    def chunk_done(part, when):
        if when == "before":
            copies[part].wait()

    _rows_cols(
        src_sm, slot_sm, lambda t, q, o: k_scr[t], chunk_done, k_scr, c_ref, r_out, colp_out, acc, rb_scr
    )


def _final_kernel(src_sm, slot_sm, k_hbm, t_ref, c_ref, r_ref, al_out, ms_out, k_scr, ms_scr, sems):
    capacity = src_sm.shape[0]
    step = _chunk(capacity)
    copies = _chunk_copies(k_hbm, k_scr, sems, capacity)
    for copy in copies:
        copy.start()
    al_out[...] = jnp.zeros_like(al_out)
    ms_scr[...] = jnp.zeros_like(ms_scr)

    def body(t, carry):
        q = src_sm[t]
        o = slot_sm[t]
        kc = k_scr[t] * c_ref[o]
        al_out[q] += jnp.dot(kc, t_ref[o], precision=HIGH, preferred_element_type=jnp.float32)
        ms_scr[q] += kc
        return carry

    for part in range(capacity // step):
        copies[part].wait()
        lax.fori_loop(part * step, (part + 1) * step, body, 0, unroll=UNROLL)
    r = r_ref[...]
    al_out[...] = al_out[...] * r * math.sqrt(E)
    for q in range(ms_out.shape[0]):
        mass = jnp.broadcast_to(jnp.sum(ms_scr[q], axis=1, keepdims=True) * r_ref[q], (BLOCK, BLOCK))
        ms_out[q : q + 1, :] = jnp.transpose(mass)[0:1, :]


def _specs(n_smem, n_vmem):
    return [pl.BlockSpec(memory_space=pltpu.SMEM)] * n_smem + [
        pl.BlockSpec(memory_space=pltpu.VMEM)
    ] * n_vmem


def _vmem_out(n):
    return (pl.BlockSpec(memory_space=pltpu.VMEM),) * n


_ANY = pl.BlockSpec(memory_space=pl.ANY)


def first_sweep(tile_source, tile_slot, live, source_unit, fetched_t, col):
    capacity = tile_source.shape[0]
    sb = source_unit.shape[0]
    slots = fetched_t.shape[0]
    return pl.pallas_call(
        _first_kernel,
        out_shape=(
            jax.ShapeDtypeStruct((capacity, BLOCK, BLOCK), jnp.float32),
            jax.ShapeDtypeStruct((sb, BLOCK, 1), jnp.float32),
            jax.ShapeDtypeStruct((slots, 1, BLOCK), jnp.float32),
        ),
        in_specs=_specs(3, 3),
        out_specs=(_ANY,) + _vmem_out(2),
        scratch_shapes=[
            pltpu.VMEM((capacity, BLOCK, BLOCK), jnp.float32),
            pltpu.VMEM((sb, BLOCK, BLOCK), jnp.float32),
            pltpu.VMEM((sb, BLOCK, BLOCK), jnp.float32),
            pltpu.SemaphoreType.DMA((capacity // _chunk(capacity),)),
        ],
    )(tile_source, tile_slot, live, source_unit, fetched_t, col)


def again_sweep(tile_source, tile_slot, kernel, col, sb):
    capacity = tile_source.shape[0]
    slots = col.shape[0]
    return pl.pallas_call(
        _again_kernel,
        out_shape=(
            jax.ShapeDtypeStruct((sb, BLOCK, 1), jnp.float32),
            jax.ShapeDtypeStruct((slots, 1, BLOCK), jnp.float32),
        ),
        in_specs=_specs(2, 0) + [_ANY] + _specs(0, 1),
        out_specs=_vmem_out(2),
        scratch_shapes=[
            pltpu.VMEM((capacity, BLOCK, BLOCK), jnp.float32),
            pltpu.VMEM((sb, BLOCK, BLOCK), jnp.float32),
            pltpu.VMEM((sb, BLOCK, BLOCK), jnp.float32),
            pltpu.SemaphoreType.DMA((capacity // _chunk(capacity),)),
        ],
    )(tile_source, tile_slot, kernel, col)


def final(tile_source, tile_slot, kernel, fetched, col, row):
    capacity = tile_source.shape[0]
    sb = row.shape[0]
    return pl.pallas_call(
        _final_kernel,
        out_shape=(
            jax.ShapeDtypeStruct((sb, BLOCK, E), jnp.float32),
            jax.ShapeDtypeStruct((sb, BLOCK), jnp.float32),
        ),
        in_specs=_specs(2, 0) + [_ANY] + _specs(0, 3),
        out_specs=_vmem_out(2),
        scratch_shapes=[
            pltpu.VMEM((capacity, BLOCK, BLOCK), jnp.float32),
            pltpu.VMEM((sb, BLOCK, BLOCK), jnp.float32),
            pltpu.SemaphoreType.DMA((capacity // _chunk(capacity),)),
        ],
    )(tile_source, tile_slot, kernel, fetched, col, row)


def on_device(source_emb, target_emb, tile_source, tile_slot, tile_count, wanted):
    rows_n = lax.axis_size("rows")
    need = wanted.shape[1]
    target_blocks = target_emb.shape[0] // BLOCK
    slots = rows_n * need
    source_unit = unit_rows(source_emb).reshape(-1, BLOCK, E)
    owners = rows_n
    wanted_row = wanted.reshape(1, slots)
    wanted_all = lax.all_to_all(
        jnp.broadcast_to(wanted_row, (rows_n, slots)), "rows", split_axis=0, concat_axis=0, tiled=True
    )
    me = lax.axis_index("rows")
    asked = lax.dynamic_slice_in_dim(wanted_all, me * need, need, axis=1)
    own_unit = unit_rows(target_emb).reshape(target_blocks, BLOCK, E)
    outgoing = own_unit[asked.reshape(-1)]
    fetched = lax.all_to_all(outgoing, "rows", split_axis=0, concat_axis=0, tiled=True)
    same_block = (
        wanted_all.reshape(rows_n, owners, need, 1) == wanted.reshape(1, owners, 1, need)
    )[..., None]

    def column_scale_of(colp):
        spread = jnp.broadcast_to(colp.reshape(1, slots, BLOCK), (rows_n, slots, BLOCK))
        gathered = lax.all_to_all(spread, "rows", split_axis=0, concat_axis=0, tiled=True)
        gathered = gathered.reshape(rows_n, owners, need, 1, BLOCK)
        totals = jnp.sum(jnp.where(same_block, gathered, 0.0), axis=(0, 2))
        return (1.0 / jnp.maximum(totals, COLUMN_FLOOR)).reshape(slots, 1, BLOCK)

    live = (jnp.arange(tile_source.shape[0]) < tile_count[0]).astype(jnp.float32)
    col = jnp.ones((slots, 1, BLOCK), jnp.float32)
    sb = source_unit.shape[0]
    fetched_t = jnp.swapaxes(fetched, 1, 2)
    kernel, row, colp = first_sweep(tile_source, tile_slot, live, source_unit, fetched_t, col)
    for iteration in range(1, ITERS):
        col = column_scale_of(colp)
        row, colp = again_sweep(tile_source, tile_slot, kernel, col, sb)
    col = column_scale_of(colp)
    al, ms = final(tile_source, tile_slot, kernel, fetched, col, row)
    return (al.reshape(-1, E), ms.reshape(-1))


def solution(mesh):
    placed = (
        P(("groups", "rows"), None),
        P(("groups", "rows"), None),
        P(("groups", "rows")),
        P(("groups", "rows")),
        P(("groups", "rows")),
        P(("groups", "rows"), None),
    )
    return jax.shard_map(
        on_device,
        mesh=mesh,
        in_specs=placed,
        out_specs=(P(("groups", "rows"), None), P(("groups", "rows"))),
        check_vma=False,
    )
```

```python
import math

import jax
import jax.numpy as jnp
from jax import lax
from jax.experimental import pallas as pl
from jax.experimental.pallas import tpu as pltpu
from jax.sharding import PartitionSpec as P

E = 128
BLOCK = 128
ITERS = 2
UNROLL = 4

EPSILON = 1e-06
SOFTMAX_WARMTH = 0.03
ROW_MINIMUM = 1.0
COLUMN_FLOOR = 0.01
HIGHEST = lax.Precision.HIGHEST
HIGH = lax.Precision.HIGH

def unit_rows(values):
    return values * lax.rsqrt(jnp.sum(values * values, axis=-1, keepdims=True) + EPSILON)


def _tile(s_ref, tt_ref, q, o):
    cosine = jnp.dot(s_ref[q], tt_ref[o], precision=HIGHEST, preferred_element_type=jnp.float32)
    return jnp.exp(cosine / SOFTMAX_WARMTH)


def _chunk(capacity):
    return math.gcd(capacity, 16)


def _rows_cols(src_sm, slot_sm, tile_at, chunk_done, k_ref, c_ref, r_out, colp_out, acc, rb_scr):
    capacity = src_sm.shape[0]
    sb = acc.shape[0]
    step = _chunk(capacity)
    acc[...] = jnp.zeros_like(acc)
    colp_out[...] = jnp.zeros_like(colp_out)

    def rows(t, carry):
        q = src_sm[t]
        o = slot_sm[t]
        acc[q] += tile_at(t, q, o) * c_ref[o]
        return carry

    for part in range(capacity // step):
        chunk_done(part, "before")
        lax.fori_loop(part * step, (part + 1) * step, rows, 0, unroll=UNROLL)
        chunk_done(part, "after")
    for q in range(sb):
        r = 1.0 / jnp.maximum(jnp.sum(acc[q], axis=1, keepdims=True), ROW_MINIMUM)
        r_out[q] = r
        rb_scr[q] = jnp.broadcast_to(r, (BLOCK, BLOCK))

    def cols(t, carry):
        q = src_sm[t]
        o = slot_sm[t]
        colp_out[o] += jnp.sum(k_ref[t] * rb_scr[q], axis=0, keepdims=True)
        return carry

    lax.fori_loop(0, capacity, cols, 0, unroll=UNROLL)


def _chunk_copies(src, dst, sems, capacity):
    step = _chunk(capacity)
    return [
        pltpu.make_async_copy(
            src.at[pl.ds(part * step, step)], dst.at[pl.ds(part * step, step)], sems.at[part]
        )
        for part in range(capacity // step)
    ]


def _first_kernel(
    src_sm, slot_sm, live_ref, s_ref, tt_ref, c_ref, k_hbm, r_out, colp_out, k_scr, acc, rb_scr, sems
):
    capacity = src_sm.shape[0]
    copies = _chunk_copies(k_scr, k_hbm, sems, capacity)

    def build(t, q, o):
        k = _tile(s_ref, tt_ref, q, o) * live_ref[t]
        k_scr[t] = k
        return k

    def chunk_done(part, when):
        if when == "after":
            copies[part].start()

    _rows_cols(src_sm, slot_sm, build, chunk_done, k_scr, c_ref, r_out, colp_out, acc, rb_scr)
    for copy in copies:
        copy.wait()


def _again_kernel(src_sm, slot_sm, k_hbm, c_ref, r_out, colp_out, k_scr, acc, rb_scr, sems):
    capacity = src_sm.shape[0]
    copies = _chunk_copies(k_hbm, k_scr, sems, capacity)
    for copy in copies:
        copy.start()

    def chunk_done(part, when):
        if when == "before":
            copies[part].wait()

    _rows_cols(
        src_sm, slot_sm, lambda t, q, o: k_scr[t], chunk_done, k_scr, c_ref, r_out, colp_out, acc, rb_scr
    )


def _final_kernel(src_sm, slot_sm, k_hbm, t_ref, c_ref, r_ref, al_out, ms_out, k_scr, ms_scr, sems):
    capacity = src_sm.shape[0]
    step = _chunk(capacity)
    copies = _chunk_copies(k_hbm, k_scr, sems, capacity)
    for copy in copies:
        copy.start()
    al_out[...] = jnp.zeros_like(al_out)
    ms_scr[...] = jnp.zeros_like(ms_scr)

    def body(t, carry):
        q = src_sm[t]
        o = slot_sm[t]
        kc = k_scr[t] * c_ref[o]
        al_out[q] += jnp.dot(kc, t_ref[o], precision=HIGH, preferred_element_type=jnp.float32)
        ms_scr[q] += kc
        return carry

    for part in range(capacity // step):
        copies[part].wait()
        lax.fori_loop(part * step, (part + 1) * step, body, 0, unroll=UNROLL)
    r = r_ref[...]
    al_out[...] = al_out[...] * r * math.sqrt(E)
    for q in range(ms_out.shape[0]):
        mass = jnp.broadcast_to(jnp.sum(ms_scr[q], axis=1, keepdims=True) * r_ref[q], (BLOCK, BLOCK))
        ms_out[q : q + 1, :] = jnp.transpose(mass)[0:1, :]


def _specs(n_smem, n_vmem):
    return [pl.BlockSpec(memory_space=pltpu.SMEM)] * n_smem + [
        pl.BlockSpec(memory_space=pltpu.VMEM)
    ] * n_vmem


def _vmem_out(n):
    return (pl.BlockSpec(memory_space=pltpu.VMEM),) * n


_ANY = pl.BlockSpec(memory_space=pl.ANY)


def first_sweep(tile_source, tile_slot, live, source_unit, fetched_t, col):
    capacity = tile_source.shape[0]
    sb = source_unit.shape[0]
    slots = fetched_t.shape[0]
    return pl.pallas_call(
        _first_kernel,
        out_shape=(
            jax.ShapeDtypeStruct((capacity, BLOCK, BLOCK), jnp.float32),
            jax.ShapeDtypeStruct((sb, BLOCK, 1), jnp.float32),
            jax.ShapeDtypeStruct((slots, 1, BLOCK), jnp.float32),
        ),
        in_specs=_specs(3, 3),
        out_specs=(_ANY,) + _vmem_out(2),
        scratch_shapes=[
            pltpu.VMEM((capacity, BLOCK, BLOCK), jnp.float32),
            pltpu.VMEM((sb, BLOCK, BLOCK), jnp.float32),
            pltpu.VMEM((sb, BLOCK, BLOCK), jnp.float32),
            pltpu.SemaphoreType.DMA((capacity // _chunk(capacity),)),
        ],
    )(tile_source, tile_slot, live, source_unit, fetched_t, col)


def again_sweep(tile_source, tile_slot, kernel, col, sb):
    capacity = tile_source.shape[0]
    slots = col.shape[0]
    return pl.pallas_call(
        _again_kernel,
        out_shape=(
            jax.ShapeDtypeStruct((sb, BLOCK, 1), jnp.float32),
            jax.ShapeDtypeStruct((slots, 1, BLOCK), jnp.float32),
        ),
        in_specs=_specs(2, 0) + [_ANY] + _specs(0, 1),
        out_specs=_vmem_out(2),
        scratch_shapes=[
            pltpu.VMEM((capacity, BLOCK, BLOCK), jnp.float32),
            pltpu.VMEM((sb, BLOCK, BLOCK), jnp.float32),
            pltpu.VMEM((sb, BLOCK, BLOCK), jnp.float32),
            pltpu.SemaphoreType.DMA((capacity // _chunk(capacity),)),
        ],
    )(tile_source, tile_slot, kernel, col)


def final(tile_source, tile_slot, kernel, fetched, col, row):
    capacity = tile_source.shape[0]
    sb = row.shape[0]
    return pl.pallas_call(
        _final_kernel,
        out_shape=(
            jax.ShapeDtypeStruct((sb, BLOCK, E), jnp.float32),
            jax.ShapeDtypeStruct((sb, BLOCK), jnp.float32),
        ),
        in_specs=_specs(2, 0) + [_ANY] + _specs(0, 3),
        out_specs=_vmem_out(2),
        scratch_shapes=[
            pltpu.VMEM((capacity, BLOCK, BLOCK), jnp.float32),
            pltpu.VMEM((sb, BLOCK, BLOCK), jnp.float32),
            pltpu.SemaphoreType.DMA((capacity // _chunk(capacity),)),
        ],
    )(tile_source, tile_slot, kernel, fetched, col, row)


def on_device(source_emb, target_emb, tile_source, tile_slot, tile_count, wanted):
    rows_n = lax.axis_size("rows")
    need = wanted.shape[1]
    target_blocks = target_emb.shape[0] // BLOCK
    slots = rows_n * need
    source_unit = unit_rows(source_emb).reshape(-1, BLOCK, E)
    owners = rows_n
    wanted_row = wanted.reshape(1, slots)
    wanted_all = lax.all_to_all(
        jnp.broadcast_to(wanted_row, (rows_n, slots)), "rows", split_axis=0, concat_axis=0, tiled=True
    )
    me = lax.axis_index("rows")
    asked = lax.dynamic_slice_in_dim(wanted_all, me * need, need, axis=1)
    own_unit = unit_rows(target_emb).reshape(target_blocks, BLOCK, E)
    outgoing = own_unit[asked.reshape(-1)]
    fetched = lax.all_to_all(outgoing, "rows", split_axis=0, concat_axis=0, tiled=True)
    same_block = (
        wanted_all.reshape(rows_n, owners, need, 1) == wanted.reshape(1, owners, 1, need)
    )[..., None]

    def column_scale_of(colp):
        spread = jnp.broadcast_to(colp.reshape(1, slots, BLOCK), (rows_n, slots, BLOCK))
        gathered = lax.all_to_all(spread, "rows", split_axis=0, concat_axis=0, tiled=True)
        gathered = gathered.reshape(rows_n, owners, need, 1, BLOCK)
        totals = jnp.sum(jnp.where(same_block, gathered, 0.0), axis=(0, 2))
        return (1.0 / jnp.maximum(totals, COLUMN_FLOOR)).reshape(slots, 1, BLOCK)

    live = (jnp.arange(tile_source.shape[0]) < tile_count[0]).astype(jnp.float32)
    col = jnp.ones((slots, 1, BLOCK), jnp.float32)
    sb = source_unit.shape[0]
    fetched_t, same_block = lax.optimization_barrier((jnp.swapaxes(fetched, 1, 2), same_block))
    kernel, row, colp = first_sweep(tile_source, tile_slot, live, source_unit, fetched_t, col)
    for iteration in range(1, ITERS):
        col = column_scale_of(colp)
        row, colp = again_sweep(tile_source, tile_slot, kernel, col, sb)
    col = column_scale_of(colp)
    al, ms = final(tile_source, tile_slot, kernel, fetched, col, row)
    return (al.reshape(-1, E), ms.reshape(-1))


def solution(mesh):
    placed = (
        P(("groups", "rows"), None),
        P(("groups", "rows"), None),
        P(("groups", "rows")),
        P(("groups", "rows")),
        P(("groups", "rows")),
        P(("groups", "rows"), None),
    )
    return jax.shard_map(
        on_device,
        mesh=mesh,
        in_specs=placed,
        out_specs=(P(("groups", "rows"), None), P(("groups", "rows"))),
        check_vma=False,
    )
```

```python
import math

import jax
import jax.numpy as jnp
from jax import lax
from jax.experimental import pallas as pl
from jax.experimental.pallas import tpu as pltpu
from jax.sharding import PartitionSpec as P

E = 128
BLOCK = 128
ITERS = 2
UNROLL = 8

EPSILON = 1e-06
SOFTMAX_WARMTH = 0.03
ROW_MINIMUM = 1.0
COLUMN_FLOOR = 0.01
HIGHEST = lax.Precision.HIGHEST
HIGH = lax.Precision.HIGH

def unit_rows(values):
    return values * lax.rsqrt(jnp.sum(values * values, axis=-1, keepdims=True) + EPSILON)


def _tile(s_ref, tt_ref, q, o):
    cosine = jnp.dot(s_ref[q], tt_ref[o], precision=HIGHEST, preferred_element_type=jnp.float32)
    return jnp.exp(cosine / SOFTMAX_WARMTH)


def _chunk(capacity):
    return math.gcd(capacity, 16)


def _rows_cols(src_sm, slot_sm, tile_at, chunk_done, k_ref, c_ref, r_out, colp_out, acc, rb_scr):
    capacity = src_sm.shape[0]
    sb = acc.shape[0]
    step = _chunk(capacity)
    acc[...] = jnp.zeros_like(acc)
    colp_out[...] = jnp.zeros_like(colp_out)

    def rows(t, carry):
        q = src_sm[t]
        o = slot_sm[t]
        if c_ref is None:
            acc[q] += tile_at(t, q, o)
        else:
            acc[q] += tile_at(t, q, o) * c_ref[o]
        return carry

    for part in range(capacity // step):
        chunk_done(part, "before")
        lax.fori_loop(part * step, (part + 1) * step, rows, 0, unroll=UNROLL)
        chunk_done(part, "after")
    for q in range(sb):
        r = 1.0 / jnp.maximum(jnp.sum(acc[q], axis=1, keepdims=True), ROW_MINIMUM)
        r_out[q] = r
        rb_scr[q] = jnp.broadcast_to(r, (BLOCK, BLOCK))

    def cols(t, carry):
        q = src_sm[t]
        o = slot_sm[t]
        colp_out[o] += jnp.sum(k_ref[t] * rb_scr[q], axis=0, keepdims=True)
        return carry

    lax.fori_loop(0, capacity, cols, 0, unroll=UNROLL)


def _chunk_copies(src, dst, sems, capacity):
    step = _chunk(capacity)
    return [
        pltpu.make_async_copy(
            src.at[pl.ds(part * step, step)], dst.at[pl.ds(part * step, step)], sems.at[part]
        )
        for part in range(capacity // step)
    ]


def _first_kernel(
    src_sm, slot_sm, live_ref, s_ref, tt_ref, c_ref, k_hbm, r_out, colp_out, k_scr, acc, rb_scr, sems
):
    capacity = src_sm.shape[0]
    copies = _chunk_copies(k_scr, k_hbm, sems, capacity)

    def build(t, q, o):
        k = _tile(s_ref, tt_ref, q, o) * live_ref[t]
        k_scr[t] = k
        return k

    def chunk_done(part, when):
        if when == "after":
            copies[part].start()

    _rows_cols(src_sm, slot_sm, build, chunk_done, k_scr, None, r_out, colp_out, acc, rb_scr)
    for copy in copies:
        copy.wait()


def _again_kernel(src_sm, slot_sm, k_hbm, c_ref, r_out, colp_out, k_scr, acc, rb_scr, sems):
    capacity = src_sm.shape[0]
    copies = _chunk_copies(k_hbm, k_scr, sems, capacity)
    for copy in copies:
        copy.start()

    def chunk_done(part, when):
        if when == "before":
            copies[part].wait()

    _rows_cols(
        src_sm, slot_sm, lambda t, q, o: k_scr[t], chunk_done, k_scr, c_ref, r_out, colp_out, acc, rb_scr
    )


def _final_kernel(src_sm, slot_sm, k_hbm, t_ref, c_ref, r_ref, al_out, ms_out, k_scr, ms_scr, sems):
    capacity = src_sm.shape[0]
    step = _chunk(capacity)
    copies = _chunk_copies(k_hbm, k_scr, sems, capacity)
    for copy in copies:
        copy.start()
    al_out[...] = jnp.zeros_like(al_out)
    ms_scr[...] = jnp.zeros_like(ms_scr)

    def body(t, carry):
        q = src_sm[t]
        o = slot_sm[t]
        kc = k_scr[t] * c_ref[o]
        al_out[q] += jnp.dot(kc, t_ref[o], precision=HIGH, preferred_element_type=jnp.float32)
        ms_scr[q] += kc
        return carry

    for part in range(capacity // step):
        copies[part].wait()
        lax.fori_loop(part * step, (part + 1) * step, body, 0, unroll=UNROLL)
    r = r_ref[...]
    al_out[...] = al_out[...] * r * math.sqrt(E)
    for q in range(ms_out.shape[0]):
        mass = jnp.broadcast_to(jnp.sum(ms_scr[q], axis=1, keepdims=True) * r_ref[q], (BLOCK, BLOCK))
        ms_out[q : q + 1, :] = jnp.transpose(mass)[0:1, :]


def _specs(n_smem, n_vmem):
    return [pl.BlockSpec(memory_space=pltpu.SMEM)] * n_smem + [
        pl.BlockSpec(memory_space=pltpu.VMEM)
    ] * n_vmem


def _vmem_out(n):
    return (pl.BlockSpec(memory_space=pltpu.VMEM),) * n


_ANY = pl.BlockSpec(memory_space=pl.ANY)


def first_sweep(tile_source, tile_slot, live, source_unit, fetched_t, col):
    capacity = tile_source.shape[0]
    sb = source_unit.shape[0]
    slots = fetched_t.shape[0]
    return pl.pallas_call(
        _first_kernel,
        out_shape=(
            jax.ShapeDtypeStruct((capacity, BLOCK, BLOCK), jnp.float32),
            jax.ShapeDtypeStruct((sb, BLOCK, 1), jnp.float32),
            jax.ShapeDtypeStruct((slots, 1, BLOCK), jnp.float32),
        ),
        in_specs=_specs(3, 3),
        out_specs=(_ANY,) + _vmem_out(2),
        scratch_shapes=[
            pltpu.VMEM((capacity, BLOCK, BLOCK), jnp.float32),
            pltpu.VMEM((sb, BLOCK, BLOCK), jnp.float32),
            pltpu.VMEM((sb, BLOCK, BLOCK), jnp.float32),
            pltpu.SemaphoreType.DMA((capacity // _chunk(capacity),)),
        ],
    )(tile_source, tile_slot, live, source_unit, fetched_t, col)


def again_sweep(tile_source, tile_slot, kernel, col, sb):
    capacity = tile_source.shape[0]
    slots = col.shape[0]
    return pl.pallas_call(
        _again_kernel,
        out_shape=(
            jax.ShapeDtypeStruct((sb, BLOCK, 1), jnp.float32),
            jax.ShapeDtypeStruct((slots, 1, BLOCK), jnp.float32),
        ),
        in_specs=_specs(2, 0) + [_ANY] + _specs(0, 1),
        out_specs=_vmem_out(2),
        scratch_shapes=[
            pltpu.VMEM((capacity, BLOCK, BLOCK), jnp.float32),
            pltpu.VMEM((sb, BLOCK, BLOCK), jnp.float32),
            pltpu.VMEM((sb, BLOCK, BLOCK), jnp.float32),
            pltpu.SemaphoreType.DMA((capacity // _chunk(capacity),)),
        ],
    )(tile_source, tile_slot, kernel, col)


def final(tile_source, tile_slot, kernel, fetched, col, row):
    capacity = tile_source.shape[0]
    sb = row.shape[0]
    return pl.pallas_call(
        _final_kernel,
        out_shape=(
            jax.ShapeDtypeStruct((sb, BLOCK, E), jnp.float32),
            jax.ShapeDtypeStruct((sb, BLOCK), jnp.float32),
        ),
        in_specs=_specs(2, 0) + [_ANY] + _specs(0, 3),
        out_specs=_vmem_out(2),
        scratch_shapes=[
            pltpu.VMEM((capacity, BLOCK, BLOCK), jnp.float32),
            pltpu.VMEM((sb, BLOCK, BLOCK), jnp.float32),
            pltpu.SemaphoreType.DMA((capacity // _chunk(capacity),)),
        ],
    )(tile_source, tile_slot, kernel, fetched, col, row)


def on_device(source_emb, target_emb, tile_source, tile_slot, tile_count, wanted):
    rows_n = lax.axis_size("rows")
    need = wanted.shape[1]
    target_blocks = target_emb.shape[0] // BLOCK
    slots = rows_n * need
    source_unit = unit_rows(source_emb).reshape(-1, BLOCK, E)
    owners = rows_n
    wanted_row = wanted.reshape(1, slots)
    wanted_all = lax.all_to_all(
        jnp.broadcast_to(wanted_row, (rows_n, slots)), "rows", split_axis=0, concat_axis=0, tiled=True
    )
    me = lax.axis_index("rows")
    asked = lax.dynamic_slice_in_dim(wanted_all, me * need, need, axis=1)
    own_unit = unit_rows(target_emb).reshape(target_blocks, BLOCK, E)
    outgoing = own_unit[asked.reshape(-1)]
    fetched = lax.all_to_all(outgoing, "rows", split_axis=0, concat_axis=0, tiled=True)
    same_block = (
        wanted_all.reshape(rows_n, owners, need, 1) == wanted.reshape(1, owners, 1, need)
    )[..., None]

    def column_scale_of(colp):
        spread = jnp.broadcast_to(colp.reshape(1, slots, BLOCK), (rows_n, slots, BLOCK))
        gathered = lax.all_to_all(spread, "rows", split_axis=0, concat_axis=0, tiled=True)
        gathered = gathered.reshape(rows_n, owners, need, 1, BLOCK)
        totals = jnp.sum(jnp.where(same_block, gathered, 0.0), axis=(0, 2))
        return (1.0 / jnp.maximum(totals, COLUMN_FLOOR)).reshape(slots, 1, BLOCK)

    live = (jnp.arange(tile_source.shape[0]) < tile_count[0]).astype(jnp.float32)
    col = jnp.ones((slots, 1, BLOCK), jnp.float32)
    sb = source_unit.shape[0]
    fetched_t, same_block = lax.optimization_barrier((jnp.swapaxes(fetched, 1, 2), same_block))
    kernel, row, colp = first_sweep(tile_source, tile_slot, live, source_unit, fetched_t, col)
    for iteration in range(1, ITERS):
        col = column_scale_of(colp)
        row, colp = again_sweep(tile_source, tile_slot, kernel, col, sb)
    col = column_scale_of(colp)
    al, ms = final(tile_source, tile_slot, kernel, fetched, col, row)
    return (al.reshape(-1, E), ms.reshape(-1))


def solution(mesh):
    placed = (
        P(("groups", "rows"), None),
        P(("groups", "rows"), None),
        P(("groups", "rows")),
        P(("groups", "rows")),
        P(("groups", "rows")),
        P(("groups", "rows"), None),
    )
    return jax.shard_map(
        on_device,
        mesh=mesh,
        in_specs=placed,
        out_specs=(P(("groups", "rows"), None), P(("groups", "rows"))),
        check_vma=False,
    )
```

```python
import math

import jax
import jax.numpy as jnp
from jax import lax
from jax.experimental import pallas as pl
from jax.experimental.pallas import tpu as pltpu
from jax.sharding import PartitionSpec as P

E = 128
BLOCK = 128
ITERS = 2
UNROLL = 16

EPSILON = 1e-06
SOFTMAX_WARMTH = 0.03
ROW_MINIMUM = 1.0
COLUMN_FLOOR = 0.01
HIGHEST = lax.Precision.HIGHEST
HIGH = lax.Precision.HIGH

def unit_rows(values):
    return values * lax.rsqrt(jnp.sum(values * values, axis=-1, keepdims=True) + EPSILON)


def _tile(s_ref, tt_ref, q, o):
    cosine = jnp.dot(s_ref[q], tt_ref[o], precision=HIGHEST, preferred_element_type=jnp.float32)
    return jnp.exp(cosine / SOFTMAX_WARMTH)


def _chunk(capacity):
    return math.gcd(capacity, 16)


def _rows_cols(src_sm, slot_sm, tile_at, chunk_done, k_ref, c_ref, r_out, colp_out, acc, rb_scr):
    capacity = src_sm.shape[0]
    sb = acc.shape[0]
    step = _chunk(capacity)
    acc[...] = jnp.zeros_like(acc)
    colp_out[...] = jnp.zeros_like(colp_out)

    def rows(t, carry):
        q = src_sm[t]
        o = slot_sm[t]
        if c_ref is None:
            acc[q] += tile_at(t, q, o)
        else:
            acc[q] += tile_at(t, q, o) * c_ref[o]
        return carry

    for part in range(capacity // step):
        chunk_done(part, "before")
        lax.fori_loop(part * step, (part + 1) * step, rows, 0, unroll=UNROLL)
        chunk_done(part, "after")
    for q in range(sb):
        r = 1.0 / jnp.maximum(jnp.sum(acc[q], axis=1, keepdims=True), ROW_MINIMUM)
        r_out[q] = r
        rb_scr[q] = jnp.broadcast_to(r, (BLOCK, BLOCK))

    def cols(t, carry):
        q = src_sm[t]
        o = slot_sm[t]
        colp_out[o] += jnp.sum(k_ref[t] * rb_scr[q], axis=0, keepdims=True)
        return carry

    lax.fori_loop(0, capacity, cols, 0, unroll=UNROLL)


def _chunk_copies(src, dst, sems, capacity):
    step = _chunk(capacity)
    return [
        pltpu.make_async_copy(
            src.at[pl.ds(part * step, step)], dst.at[pl.ds(part * step, step)], sems.at[part]
        )
        for part in range(capacity // step)
    ]


def _first_kernel(
    src_sm, slot_sm, live_ref, s_ref, tt_ref, c_ref, k_hbm, r_out, colp_out, k_scr, acc, rb_scr, sems
):
    capacity = src_sm.shape[0]
    copies = _chunk_copies(k_scr, k_hbm, sems, capacity)

    def build(t, q, o):
        k = _tile(s_ref, tt_ref, q, o) * live_ref[t]
        k_scr[t] = k
        return k

    def chunk_done(part, when):
        if when == "after":
            copies[part].start()

    _rows_cols(src_sm, slot_sm, build, chunk_done, k_scr, None, r_out, colp_out, acc, rb_scr)
    for copy in copies:
        copy.wait()


def _again_kernel(src_sm, slot_sm, k_hbm, c_ref, r_out, colp_out, k_scr, acc, rb_scr, sems):
    capacity = src_sm.shape[0]
    copies = _chunk_copies(k_hbm, k_scr, sems, capacity)
    for copy in copies:
        copy.start()

    def chunk_done(part, when):
        if when == "before":
            copies[part].wait()

    _rows_cols(
        src_sm, slot_sm, lambda t, q, o: k_scr[t], chunk_done, k_scr, c_ref, r_out, colp_out, acc, rb_scr
    )


def _final_kernel(src_sm, slot_sm, k_hbm, t_ref, c_ref, r_ref, al_out, ms_out, k_scr, ms_scr, sems):
    capacity = src_sm.shape[0]
    step = _chunk(capacity)
    copies = _chunk_copies(k_hbm, k_scr, sems, capacity)
    for copy in copies:
        copy.start()
    al_out[...] = jnp.zeros_like(al_out)
    ms_scr[...] = jnp.zeros_like(ms_scr)

    def body(t, carry):
        q = src_sm[t]
        o = slot_sm[t]
        kc = k_scr[t] * c_ref[o]
        al_out[q] += jnp.dot(kc, t_ref[o], precision=HIGH, preferred_element_type=jnp.float32)
        ms_scr[q] += kc
        return carry

    for part in range(capacity // step):
        copies[part].wait()
        lax.fori_loop(part * step, (part + 1) * step, body, 0, unroll=UNROLL)
    r = r_ref[...]
    al_out[...] = al_out[...] * r * math.sqrt(E)
    for q in range(ms_out.shape[0]):
        mass = jnp.broadcast_to(jnp.sum(ms_scr[q], axis=1, keepdims=True) * r_ref[q], (BLOCK, BLOCK))
        ms_out[q : q + 1, :] = jnp.transpose(mass)[0:1, :]


def _specs(n_smem, n_vmem):
    return [pl.BlockSpec(memory_space=pltpu.SMEM)] * n_smem + [
        pl.BlockSpec(memory_space=pltpu.VMEM)
    ] * n_vmem


def _vmem_out(n):
    return (pl.BlockSpec(memory_space=pltpu.VMEM),) * n


_ANY = pl.BlockSpec(memory_space=pl.ANY)


def first_sweep(tile_source, tile_slot, live, source_unit, fetched_t, col):
    capacity = tile_source.shape[0]
    sb = source_unit.shape[0]
    slots = fetched_t.shape[0]
    return pl.pallas_call(
        _first_kernel,
        out_shape=(
            jax.ShapeDtypeStruct((capacity, BLOCK, BLOCK), jnp.float32),
            jax.ShapeDtypeStruct((sb, BLOCK, 1), jnp.float32),
            jax.ShapeDtypeStruct((slots, 1, BLOCK), jnp.float32),
        ),
        in_specs=_specs(3, 3),
        out_specs=(_ANY,) + _vmem_out(2),
        scratch_shapes=[
            pltpu.VMEM((capacity, BLOCK, BLOCK), jnp.float32),
            pltpu.VMEM((sb, BLOCK, BLOCK), jnp.float32),
            pltpu.VMEM((sb, BLOCK, BLOCK), jnp.float32),
            pltpu.SemaphoreType.DMA((capacity // _chunk(capacity),)),
        ],
    )(tile_source, tile_slot, live, source_unit, fetched_t, col)


def again_sweep(tile_source, tile_slot, kernel, col, sb):
    capacity = tile_source.shape[0]
    slots = col.shape[0]
    return pl.pallas_call(
        _again_kernel,
        out_shape=(
            jax.ShapeDtypeStruct((sb, BLOCK, 1), jnp.float32),
            jax.ShapeDtypeStruct((slots, 1, BLOCK), jnp.float32),
        ),
        in_specs=_specs(2, 0) + [_ANY] + _specs(0, 1),
        out_specs=_vmem_out(2),
        scratch_shapes=[
            pltpu.VMEM((capacity, BLOCK, BLOCK), jnp.float32),
            pltpu.VMEM((sb, BLOCK, BLOCK), jnp.float32),
            pltpu.VMEM((sb, BLOCK, BLOCK), jnp.float32),
            pltpu.SemaphoreType.DMA((capacity // _chunk(capacity),)),
        ],
    )(tile_source, tile_slot, kernel, col)


def final(tile_source, tile_slot, kernel, fetched, col, row):
    capacity = tile_source.shape[0]
    sb = row.shape[0]
    return pl.pallas_call(
        _final_kernel,
        out_shape=(
            jax.ShapeDtypeStruct((sb, BLOCK, E), jnp.float32),
            jax.ShapeDtypeStruct((sb, BLOCK), jnp.float32),
        ),
        in_specs=_specs(2, 0) + [_ANY] + _specs(0, 3),
        out_specs=_vmem_out(2),
        scratch_shapes=[
            pltpu.VMEM((capacity, BLOCK, BLOCK), jnp.float32),
            pltpu.VMEM((sb, BLOCK, BLOCK), jnp.float32),
            pltpu.SemaphoreType.DMA((capacity // _chunk(capacity),)),
        ],
    )(tile_source, tile_slot, kernel, fetched, col, row)


def on_device(source_emb, target_emb, tile_source, tile_slot, tile_count, wanted):
    rows_n = lax.axis_size("rows")
    need = wanted.shape[1]
    target_blocks = target_emb.shape[0] // BLOCK
    slots = rows_n * need
    source_unit = unit_rows(source_emb).reshape(-1, BLOCK, E)
    owners = rows_n
    wanted_row = wanted.reshape(1, slots)
    wanted_all = lax.all_to_all(
        jnp.broadcast_to(wanted_row, (rows_n, slots)), "rows", split_axis=0, concat_axis=0, tiled=True
    )
    me = lax.axis_index("rows")
    asked = lax.dynamic_slice_in_dim(wanted_all, me * need, need, axis=1)
    own_unit = unit_rows(target_emb).reshape(target_blocks, BLOCK, E)
    outgoing = own_unit[asked.reshape(-1)]
    fetched = lax.all_to_all(outgoing, "rows", split_axis=0, concat_axis=0, tiled=True)
    same_block = (
        wanted_all.reshape(rows_n, owners, need, 1) == wanted.reshape(1, owners, 1, need)
    )[..., None]

    def column_scale_of(colp):
        spread = jnp.broadcast_to(colp.reshape(1, slots, BLOCK), (rows_n, slots, BLOCK))
        gathered = lax.all_to_all(spread, "rows", split_axis=0, concat_axis=0, tiled=True)
        gathered = gathered.reshape(rows_n, owners, need, 1, BLOCK)
        totals = jnp.sum(jnp.where(same_block, gathered, 0.0), axis=(0, 2))
        return (1.0 / jnp.maximum(totals, COLUMN_FLOOR)).reshape(slots, 1, BLOCK)

    live = (jnp.arange(tile_source.shape[0]) < tile_count[0]).astype(jnp.float32)
    col = jnp.ones((slots, 1, BLOCK), jnp.float32)
    sb = source_unit.shape[0]
    fetched_t, same_block = lax.optimization_barrier((jnp.swapaxes(fetched, 1, 2), same_block))
    kernel, row, colp = first_sweep(tile_source, tile_slot, live, source_unit, fetched_t, col)
    for iteration in range(1, ITERS):
        col = column_scale_of(colp)
        row, colp = again_sweep(tile_source, tile_slot, kernel, col, sb)
    col = column_scale_of(colp)
    al, ms = final(tile_source, tile_slot, kernel, fetched, col, row)
    return (al.reshape(-1, E), ms.reshape(-1))


def solution(mesh):
    placed = (
        P(("groups", "rows"), None),
        P(("groups", "rows"), None),
        P(("groups", "rows")),
        P(("groups", "rows")),
        P(("groups", "rows")),
        P(("groups", "rows"), None),
    )
    return jax.shard_map(
        on_device,
        mesh=mesh,
        in_specs=placed,
        out_specs=(P(("groups", "rows"), None), P(("groups", "rows"))),
        check_vma=False,
    )
```

```python
import math

import jax
import jax.numpy as jnp
from jax import lax
from jax.experimental import pallas as pl
from jax.experimental.pallas import tpu as pltpu
from jax.sharding import PartitionSpec as P

E = 128
BLOCK = 128
ITERS = 2
UNROLL = 16

EPSILON = 1e-06
SOFTMAX_WARMTH = 0.03
ROW_MINIMUM = 1.0
COLUMN_FLOOR = 0.01
HIGHEST = lax.Precision.HIGHEST
HIGH = lax.Precision.HIGH

def unit_rows(values):
    return values * lax.rsqrt(jnp.sum(values * values, axis=-1, keepdims=True) + EPSILON)


def _tile(s_ref, tt_ref, q, o):
    cosine = jnp.dot(s_ref[q], tt_ref[o], precision=HIGHEST, preferred_element_type=jnp.float32)
    return jnp.exp(cosine / SOFTMAX_WARMTH)


def _chunk(capacity):
    return math.gcd(capacity, 16)


def _rows_cols(src_sm, slot_sm, tile_at, chunk_done, k_ref, c_ref, r_out, spread_out, acc, rb_scr, colp_out):
    capacity = src_sm.shape[0]
    sb = acc.shape[0]
    step = _chunk(capacity)
    acc[...] = jnp.zeros_like(acc)
    colp_out[...] = jnp.zeros_like(colp_out)

    def rows(t, carry):
        q = src_sm[t]
        o = slot_sm[t]
        if c_ref is None:
            acc[q] += tile_at(t, q, o)
        else:
            acc[q] += tile_at(t, q, o) * c_ref[o]
        return carry

    for part in range(capacity // step):
        chunk_done(part, "before")
        lax.fori_loop(part * step, (part + 1) * step, rows, 0, unroll=UNROLL)
        chunk_done(part, "after")
    for q in range(sb):
        r = 1.0 / jnp.maximum(jnp.sum(acc[q], axis=1, keepdims=True), ROW_MINIMUM)
        r_out[q] = r
        rb_scr[q] = jnp.broadcast_to(r, (BLOCK, BLOCK))

    def cols(t, carry):
        q = src_sm[t]
        o = slot_sm[t]
        colp_out[o] += jnp.sum(k_ref[t] * rb_scr[q], axis=0, keepdims=True)
        return carry

    lax.fori_loop(0, capacity, cols, 0, unroll=UNROLL)
    partials = jnp.concatenate([colp_out[o] for o in range(colp_out.shape[0])], axis=0)
    for d in range(spread_out.shape[0]):
        spread_out[d] = partials


def _chunk_copies(src, dst, sems, capacity):
    step = _chunk(capacity)
    return [
        pltpu.make_async_copy(
            src.at[pl.ds(part * step, step)], dst.at[pl.ds(part * step, step)], sems.at[part]
        )
        for part in range(capacity // step)
    ]


def _first_kernel(
    src_sm, slot_sm, live_ref, s_ref, tt_ref, k_hbm, r_out, spread_out, k_scr, acc, rb_scr, colp, sems
):
    capacity = src_sm.shape[0]
    copies = _chunk_copies(k_scr, k_hbm, sems, capacity)

    def build(t, q, o):
        k = _tile(s_ref, tt_ref, q, o) * live_ref[t]
        k_scr[t] = k
        return k

    def chunk_done(part, when):
        if when == "after":
            copies[part].start()

    _rows_cols(src_sm, slot_sm, build, chunk_done, k_scr, None, r_out, spread_out, acc, rb_scr, colp)
    for copy in copies:
        copy.wait()


def _again_kernel(src_sm, slot_sm, k_hbm, c_ref, r_out, spread_out, k_scr, acc, rb_scr, colp, sems):
    capacity = src_sm.shape[0]
    copies = _chunk_copies(k_hbm, k_scr, sems, capacity)
    for copy in copies:
        copy.start()

    def chunk_done(part, when):
        if when == "before":
            copies[part].wait()

    _rows_cols(
        src_sm,
        slot_sm,
        lambda t, q, o: k_scr[t],
        chunk_done,
        k_scr,
        c_ref,
        r_out,
        spread_out,
        acc,
        rb_scr,
        colp,
    )


def _final_kernel(src_sm, slot_sm, k_hbm, t_ref, c_ref, r_ref, al_out, ms_out, k_scr, ms_scr, sems):
    capacity = src_sm.shape[0]
    step = _chunk(capacity)
    copies = _chunk_copies(k_hbm, k_scr, sems, capacity)
    for copy in copies:
        copy.start()
    al_out[...] = jnp.zeros_like(al_out)
    ms_scr[...] = jnp.zeros_like(ms_scr)

    def body(t, carry):
        q = src_sm[t]
        o = slot_sm[t]
        kc = k_scr[t] * c_ref[o]
        al_out[q] += jnp.dot(kc, t_ref[o], precision=HIGH, preferred_element_type=jnp.float32)
        ms_scr[q] += kc
        return carry

    for part in range(capacity // step):
        copies[part].wait()
        lax.fori_loop(part * step, (part + 1) * step, body, 0, unroll=UNROLL)
    r = r_ref[...]
    al_out[...] = al_out[...] * r * math.sqrt(E)
    for q in range(ms_out.shape[0]):
        mass = jnp.broadcast_to(jnp.sum(ms_scr[q], axis=1, keepdims=True) * r_ref[q], (BLOCK, BLOCK))
        ms_out[q : q + 1, :] = jnp.transpose(mass)[0:1, :]


def _specs(n_smem, n_vmem):
    return [pl.BlockSpec(memory_space=pltpu.SMEM)] * n_smem + [
        pl.BlockSpec(memory_space=pltpu.VMEM)
    ] * n_vmem


def _vmem_out(n):
    return (pl.BlockSpec(memory_space=pltpu.VMEM),) * n


_ANY = pl.BlockSpec(memory_space=pl.ANY)


def first_sweep(tile_source, tile_slot, live, source_unit, fetched_t, rows_n):
    capacity = tile_source.shape[0]
    sb = source_unit.shape[0]
    slots = fetched_t.shape[0]
    return pl.pallas_call(
        _first_kernel,
        out_shape=(
            jax.ShapeDtypeStruct((capacity, BLOCK, BLOCK), jnp.float32),
            jax.ShapeDtypeStruct((sb, BLOCK, 1), jnp.float32),
            jax.ShapeDtypeStruct((rows_n, slots, BLOCK), jnp.float32),
        ),
        in_specs=_specs(3, 2),
        out_specs=(_ANY,) + _vmem_out(2),
        scratch_shapes=[
            pltpu.VMEM((capacity, BLOCK, BLOCK), jnp.float32),
            pltpu.VMEM((sb, BLOCK, BLOCK), jnp.float32),
            pltpu.VMEM((sb, BLOCK, BLOCK), jnp.float32),
            pltpu.VMEM((slots, 1, BLOCK), jnp.float32),
            pltpu.SemaphoreType.DMA((capacity // _chunk(capacity),)),
        ],
    )(tile_source, tile_slot, live, source_unit, fetched_t)


def again_sweep(tile_source, tile_slot, kernel, col, sb, rows_n):
    capacity = tile_source.shape[0]
    slots = col.shape[0]
    return pl.pallas_call(
        _again_kernel,
        out_shape=(
            jax.ShapeDtypeStruct((sb, BLOCK, 1), jnp.float32),
            jax.ShapeDtypeStruct((rows_n, slots, BLOCK), jnp.float32),
        ),
        in_specs=_specs(2, 0) + [_ANY] + _specs(0, 1),
        out_specs=_vmem_out(2),
        scratch_shapes=[
            pltpu.VMEM((capacity, BLOCK, BLOCK), jnp.float32),
            pltpu.VMEM((sb, BLOCK, BLOCK), jnp.float32),
            pltpu.VMEM((sb, BLOCK, BLOCK), jnp.float32),
            pltpu.VMEM((slots, 1, BLOCK), jnp.float32),
            pltpu.SemaphoreType.DMA((capacity // _chunk(capacity),)),
        ],
    )(tile_source, tile_slot, kernel, col)


def final(tile_source, tile_slot, kernel, fetched, col, row):
    capacity = tile_source.shape[0]
    sb = row.shape[0]
    return pl.pallas_call(
        _final_kernel,
        out_shape=(
            jax.ShapeDtypeStruct((sb, BLOCK, E), jnp.float32),
            jax.ShapeDtypeStruct((sb, BLOCK), jnp.float32),
        ),
        in_specs=_specs(2, 0) + [_ANY] + _specs(0, 3),
        out_specs=_vmem_out(2),
        scratch_shapes=[
            pltpu.VMEM((capacity, BLOCK, BLOCK), jnp.float32),
            pltpu.VMEM((sb, BLOCK, BLOCK), jnp.float32),
            pltpu.SemaphoreType.DMA((capacity // _chunk(capacity),)),
        ],
    )(tile_source, tile_slot, kernel, fetched, col, row)


def on_device(source_emb, target_emb, tile_source, tile_slot, tile_count, wanted):
    rows_n = lax.axis_size("rows")
    need = wanted.shape[1]
    target_blocks = target_emb.shape[0] // BLOCK
    slots = rows_n * need
    source_unit = unit_rows(source_emb).reshape(-1, BLOCK, E)
    owners = rows_n
    wanted_row = wanted.reshape(1, slots)
    wanted_all = lax.all_to_all(
        jnp.broadcast_to(wanted_row, (rows_n, slots)), "rows", split_axis=0, concat_axis=0, tiled=True
    )
    me = lax.axis_index("rows")
    asked = lax.dynamic_slice_in_dim(wanted_all, me * need, need, axis=1)
    own_unit = unit_rows(target_emb).reshape(target_blocks, BLOCK, E)
    outgoing = own_unit[asked.reshape(-1)]
    fetched = lax.all_to_all(outgoing, "rows", split_axis=0, concat_axis=0, tiled=True)
    same_block = (
        wanted_all.reshape(rows_n, owners, need, 1) == wanted.reshape(1, owners, 1, need)
    )[..., None]

    def column_scale_of(spread):
        gathered = lax.all_to_all(spread, "rows", split_axis=0, concat_axis=0, tiled=True)
        gathered = gathered.reshape(rows_n, owners, need, 1, BLOCK)
        totals = jnp.sum(jnp.where(same_block, gathered, 0.0), axis=(0, 2))
        return (1.0 / jnp.maximum(totals, COLUMN_FLOOR)).reshape(slots, 1, BLOCK)

    live = (jnp.arange(tile_source.shape[0]) < tile_count[0]).astype(jnp.float32)
    sb = source_unit.shape[0]
    fetched_t, same_block = lax.optimization_barrier((jnp.swapaxes(fetched, 1, 2), same_block))
    kernel, row, colp = first_sweep(tile_source, tile_slot, live, source_unit, fetched_t, rows_n)
    for iteration in range(1, ITERS):
        col = column_scale_of(colp)
        row, colp = again_sweep(tile_source, tile_slot, kernel, col, sb, rows_n)
    col = column_scale_of(colp)
    al, ms = final(tile_source, tile_slot, kernel, fetched, col, row)
    return (al.reshape(-1, E), ms.reshape(-1))


def solution(mesh):
    placed = (
        P(("groups", "rows"), None),
        P(("groups", "rows"), None),
        P(("groups", "rows")),
        P(("groups", "rows")),
        P(("groups", "rows")),
        P(("groups", "rows"), None),
    )
    return jax.shard_map(
        on_device,
        mesh=mesh,
        in_specs=placed,
        out_specs=(P(("groups", "rows"), None), P(("groups", "rows"))),
        check_vma=False,
    )
```

```python
import math

import jax
import jax.numpy as jnp
from jax import lax
from jax.experimental import pallas as pl
from jax.experimental.pallas import tpu as pltpu
from jax.sharding import PartitionSpec as P

E = 128
BLOCK = 128
ITERS = 2
UNROLL = 32

EPSILON = 1e-06
SOFTMAX_WARMTH = 0.03
ROW_MINIMUM = 1.0
COLUMN_FLOOR = 0.01
HIGHEST = lax.Precision.HIGHEST
HIGH = lax.Precision.HIGH

def unit_rows(values):
    return values * lax.rsqrt(jnp.sum(values * values, axis=-1, keepdims=True) + EPSILON)


def _tile(s_ref, tt_ref, q, o):
    cosine = jnp.dot(s_ref[q], tt_ref[o], precision=HIGHEST, preferred_element_type=jnp.float32)
    return jnp.exp(cosine / SOFTMAX_WARMTH)


def _chunk(capacity):
    return math.gcd(capacity, 32)


def _rows_cols(src_sm, slot_sm, tile_at, chunk_done, k_ref, c_ref, r_out, spread_out, acc, rb_scr, colp_out):
    capacity = src_sm.shape[0]
    sb = acc.shape[0]
    step = _chunk(capacity)
    acc[...] = jnp.zeros_like(acc)
    colp_out[...] = jnp.zeros_like(colp_out)

    def rows(t, carry):
        q = src_sm[t]
        o = slot_sm[t]
        if c_ref is None:
            acc[q] += tile_at(t, q, o)
        else:
            acc[q] += tile_at(t, q, o) * c_ref[o]
        return carry

    for part in range(capacity // step):
        chunk_done(part, "before")
        lax.fori_loop(part * step, (part + 1) * step, rows, 0, unroll=UNROLL)
        chunk_done(part, "after")
    for q in range(sb):
        r = 1.0 / jnp.maximum(jnp.sum(acc[q], axis=1, keepdims=True), ROW_MINIMUM)
        r_out[q] = r
        rb_scr[q] = jnp.broadcast_to(r, (BLOCK, BLOCK))

    def cols(t, carry):
        q = src_sm[t]
        o = slot_sm[t]
        colp_out[o] += jnp.sum(k_ref[t] * rb_scr[q], axis=0, keepdims=True)
        return carry

    lax.fori_loop(0, capacity, cols, 0, unroll=UNROLL)
    partials = jnp.concatenate([colp_out[o] for o in range(colp_out.shape[0])], axis=0)
    for d in range(spread_out.shape[0]):
        spread_out[d] = partials


def _chunk_copies(src, dst, sems, capacity):
    step = _chunk(capacity)
    return [
        pltpu.make_async_copy(
            src.at[pl.ds(part * step, step)], dst.at[pl.ds(part * step, step)], sems.at[part]
        )
        for part in range(capacity // step)
    ]


def _first_kernel(
    src_sm, slot_sm, live_ref, s_ref, tt_ref, k_hbm, r_out, spread_out, k_scr, acc, rb_scr, colp, sems
):
    capacity = src_sm.shape[0]
    copies = _chunk_copies(k_scr, k_hbm, sems, capacity)

    def build(t, q, o):
        k = _tile(s_ref, tt_ref, q, o) * live_ref[t]
        k_scr[t] = k
        return k

    def chunk_done(part, when):
        if when == "after":
            copies[part].start()

    _rows_cols(src_sm, slot_sm, build, chunk_done, k_scr, None, r_out, spread_out, acc, rb_scr, colp)
    for copy in copies:
        copy.wait()


def _again_kernel(src_sm, slot_sm, k_hbm, c_ref, r_out, spread_out, k_scr, acc, rb_scr, colp, sems):
    capacity = src_sm.shape[0]
    copies = _chunk_copies(k_hbm, k_scr, sems, capacity)
    for copy in copies:
        copy.start()

    def chunk_done(part, when):
        if when == "before":
            copies[part].wait()

    _rows_cols(
        src_sm,
        slot_sm,
        lambda t, q, o: k_scr[t],
        chunk_done,
        k_scr,
        c_ref,
        r_out,
        spread_out,
        acc,
        rb_scr,
        colp,
    )


def _final_kernel(src_sm, slot_sm, k_hbm, t_ref, c_ref, r_ref, al_out, ms_out, k_scr, ms_scr, sems):
    capacity = src_sm.shape[0]
    step = _chunk(capacity)
    copies = _chunk_copies(k_hbm, k_scr, sems, capacity)
    for copy in copies:
        copy.start()
    al_out[...] = jnp.zeros_like(al_out)
    ms_scr[...] = jnp.zeros_like(ms_scr)

    def body(t, carry):
        q = src_sm[t]
        o = slot_sm[t]
        kc = k_scr[t] * c_ref[o]
        al_out[q] += jnp.dot(kc, t_ref[o], precision=HIGH, preferred_element_type=jnp.float32)
        ms_scr[q] += kc
        return carry

    for part in range(capacity // step):
        copies[part].wait()
        lax.fori_loop(part * step, (part + 1) * step, body, 0, unroll=UNROLL)
    r = r_ref[...]
    al_out[...] = al_out[...] * r * math.sqrt(E)
    for q in range(ms_out.shape[0]):
        mass = jnp.broadcast_to(jnp.sum(ms_scr[q], axis=1, keepdims=True) * r_ref[q], (BLOCK, BLOCK))
        ms_out[q : q + 1, :] = jnp.transpose(mass)[0:1, :]


def _specs(n_smem, n_vmem):
    return [pl.BlockSpec(memory_space=pltpu.SMEM)] * n_smem + [
        pl.BlockSpec(memory_space=pltpu.VMEM)
    ] * n_vmem


def _vmem_out(n):
    return (pl.BlockSpec(memory_space=pltpu.VMEM),) * n


_ANY = pl.BlockSpec(memory_space=pl.ANY)


def first_sweep(tile_source, tile_slot, live, source_unit, fetched_t, rows_n):
    capacity = tile_source.shape[0]
    sb = source_unit.shape[0]
    slots = fetched_t.shape[0]
    return pl.pallas_call(
        _first_kernel,
        out_shape=(
            jax.ShapeDtypeStruct((capacity, BLOCK, BLOCK), jnp.float32),
            jax.ShapeDtypeStruct((sb, BLOCK, 1), jnp.float32),
            jax.ShapeDtypeStruct((rows_n, slots, BLOCK), jnp.float32),
        ),
        in_specs=_specs(3, 2),
        out_specs=(_ANY,) + _vmem_out(2),
        scratch_shapes=[
            pltpu.VMEM((capacity, BLOCK, BLOCK), jnp.float32),
            pltpu.VMEM((sb, BLOCK, BLOCK), jnp.float32),
            pltpu.VMEM((sb, BLOCK, BLOCK), jnp.float32),
            pltpu.VMEM((slots, 1, BLOCK), jnp.float32),
            pltpu.SemaphoreType.DMA((capacity // _chunk(capacity),)),
        ],
    )(tile_source, tile_slot, live, source_unit, fetched_t)


def again_sweep(tile_source, tile_slot, kernel, col, sb, rows_n):
    capacity = tile_source.shape[0]
    slots = col.shape[0]
    return pl.pallas_call(
        _again_kernel,
        out_shape=(
            jax.ShapeDtypeStruct((sb, BLOCK, 1), jnp.float32),
            jax.ShapeDtypeStruct((rows_n, slots, BLOCK), jnp.float32),
        ),
        in_specs=_specs(2, 0) + [_ANY] + _specs(0, 1),
        out_specs=_vmem_out(2),
        scratch_shapes=[
            pltpu.VMEM((capacity, BLOCK, BLOCK), jnp.float32),
            pltpu.VMEM((sb, BLOCK, BLOCK), jnp.float32),
            pltpu.VMEM((sb, BLOCK, BLOCK), jnp.float32),
            pltpu.VMEM((slots, 1, BLOCK), jnp.float32),
            pltpu.SemaphoreType.DMA((capacity // _chunk(capacity),)),
        ],
    )(tile_source, tile_slot, kernel, col)


def final(tile_source, tile_slot, kernel, fetched, col, row):
    capacity = tile_source.shape[0]
    sb = row.shape[0]
    return pl.pallas_call(
        _final_kernel,
        out_shape=(
            jax.ShapeDtypeStruct((sb, BLOCK, E), jnp.float32),
            jax.ShapeDtypeStruct((sb, BLOCK), jnp.float32),
        ),
        in_specs=_specs(2, 0) + [_ANY] + _specs(0, 3),
        out_specs=_vmem_out(2),
        scratch_shapes=[
            pltpu.VMEM((capacity, BLOCK, BLOCK), jnp.float32),
            pltpu.VMEM((sb, BLOCK, BLOCK), jnp.float32),
            pltpu.SemaphoreType.DMA((capacity // _chunk(capacity),)),
        ],
    )(tile_source, tile_slot, kernel, fetched, col, row)


def on_device(source_emb, target_emb, tile_source, tile_slot, tile_count, wanted):
    rows_n = lax.axis_size("rows")
    need = wanted.shape[1]
    target_blocks = target_emb.shape[0] // BLOCK
    slots = rows_n * need
    source_unit = unit_rows(source_emb).reshape(-1, BLOCK, E)
    owners = rows_n
    wanted_row = wanted.reshape(1, slots)
    wanted_all = lax.all_to_all(
        jnp.broadcast_to(wanted_row, (rows_n, slots)), "rows", split_axis=0, concat_axis=0, tiled=True
    )
    me = lax.axis_index("rows")
    asked = lax.dynamic_slice_in_dim(wanted_all, me * need, need, axis=1)
    own_unit = unit_rows(target_emb).reshape(target_blocks, BLOCK, E)
    outgoing = own_unit[asked.reshape(-1)]
    fetched = lax.all_to_all(outgoing, "rows", split_axis=0, concat_axis=0, tiled=True)
    same_block = (
        wanted_all.reshape(rows_n, owners, need, 1) == wanted.reshape(1, owners, 1, need)
    )[..., None]

    def column_scale_of(spread):
        gathered = lax.all_to_all(spread, "rows", split_axis=0, concat_axis=0, tiled=True)
        gathered = gathered.reshape(rows_n, owners, need, 1, BLOCK)
        totals = jnp.sum(jnp.where(same_block, gathered, 0.0), axis=(0, 2))
        return (1.0 / jnp.maximum(totals, COLUMN_FLOOR)).reshape(slots, 1, BLOCK)

    live = (jnp.arange(tile_source.shape[0]) < tile_count[0]).astype(jnp.float32)
    sb = source_unit.shape[0]
    fetched_t, same_block = lax.optimization_barrier((jnp.swapaxes(fetched, 1, 2), same_block))
    kernel, row, colp = first_sweep(tile_source, tile_slot, live, source_unit, fetched_t, rows_n)
    for iteration in range(1, ITERS):
        col = column_scale_of(colp)
        row, colp = again_sweep(tile_source, tile_slot, kernel, col, sb, rows_n)
    col = column_scale_of(colp)
    al, ms = final(tile_source, tile_slot, kernel, fetched, col, row)
    return (al.reshape(-1, E), ms.reshape(-1))


def solution(mesh):
    placed = (
        P(("groups", "rows"), None),
        P(("groups", "rows"), None),
        P(("groups", "rows")),
        P(("groups", "rows")),
        P(("groups", "rows")),
        P(("groups", "rows"), None),
    )
    return jax.shard_map(
        on_device,
        mesh=mesh,
        in_specs=placed,
        out_specs=(P(("groups", "rows"), None), P(("groups", "rows"))),
        check_vma=False,
    )
```

```python
import math

import jax
import jax.numpy as jnp
from jax import lax
from jax.experimental import pallas as pl
from jax.experimental.pallas import tpu as pltpu
from jax.sharding import PartitionSpec as P

E = 128
BLOCK = 128
ITERS = 2
UNROLL = 32

EPSILON = 1e-06
SOFTMAX_WARMTH = 0.03
ROW_MINIMUM = 1.0
COLUMN_FLOOR = 0.01
HIGHEST = lax.Precision.HIGHEST
HIGH = lax.Precision.HIGH

def unit_rows(values):
    return values * lax.rsqrt(jnp.sum(values * values, axis=-1, keepdims=True) + EPSILON)


def _tile(s_ref, tt_ref, q, o):
    cosine = jnp.dot(s_ref[q], tt_ref[o], precision=HIGHEST, preferred_element_type=jnp.float32)
    return jnp.exp(cosine / SOFTMAX_WARMTH)


def _chunk(capacity):
    return math.gcd(capacity, 32)


def _rows_cols(src_sm, slot_sm, tile_at, chunk_done, k_ref, c_ref, r_out, spread_out, acc, rb_scr, colp_out):
    capacity = src_sm.shape[0]
    sb = acc.shape[0]
    step = _chunk(capacity)
    acc[...] = jnp.zeros_like(acc)
    colp_out[...] = jnp.zeros_like(colp_out)

    def rows(t, carry):
        q = src_sm[t]
        o = slot_sm[t]
        if c_ref is None:
            acc[q] += tile_at(t, q, o)
        else:
            acc[q] += tile_at(t, q, o) * c_ref[o]
        return carry

    for part in range(capacity // step):
        chunk_done(part, "before")
        lax.fori_loop(part * step, (part + 1) * step, rows, 0, unroll=UNROLL)
        chunk_done(part, "after")
    for q in range(sb):
        r = 1.0 / jnp.maximum(jnp.sum(acc[q], axis=1, keepdims=True), ROW_MINIMUM)
        r_out[q] = r
        rb_scr[q] = jnp.broadcast_to(r, (BLOCK, BLOCK))

    def cols(t, carry):
        q = src_sm[t]
        o = slot_sm[t]
        colp_out[o] += jnp.sum(k_ref[t] * rb_scr[q], axis=0, keepdims=True)
        return carry

    lax.fori_loop(0, capacity, cols, 0, unroll=UNROLL)
    partials = jnp.concatenate([colp_out[o] for o in range(colp_out.shape[0])], axis=0)
    for d in range(spread_out.shape[0]):
        spread_out[d] = partials


def _chunk_copies(src, dst, sems, capacity):
    step = _chunk(capacity)
    return [
        pltpu.make_async_copy(
            src.at[pl.ds(part * step, step)], dst.at[pl.ds(part * step, step)], sems.at[part]
        )
        for part in range(capacity // step)
    ]


def _first_kernel(
    src_sm, slot_sm, live_ref, s_ref, tt_ref, k_hbm, r_out, spread_out, k_scr, acc, rb_scr, colp, sems
):
    capacity = src_sm.shape[0]
    copies = _chunk_copies(k_scr, k_hbm, sems, capacity)

    def build(t, q, o):
        k = _tile(s_ref, tt_ref, q, o) * live_ref[t]
        k_scr[t] = k
        return k

    def chunk_done(part, when):
        if when == "after":
            copies[part].start()

    _rows_cols(src_sm, slot_sm, build, chunk_done, k_scr, None, r_out, spread_out, acc, rb_scr, colp)
    for copy in copies:
        copy.wait()


def _again_kernel(src_sm, slot_sm, k_hbm, c_ref, r_out, spread_out, k_scr, acc, rb_scr, colp, sems):
    capacity = src_sm.shape[0]
    copies = _chunk_copies(k_hbm, k_scr, sems, capacity)
    for copy in copies:
        copy.start()

    def chunk_done(part, when):
        if when == "before":
            copies[part].wait()

    _rows_cols(
        src_sm,
        slot_sm,
        lambda t, q, o: k_scr[t],
        chunk_done,
        k_scr,
        c_ref,
        r_out,
        spread_out,
        acc,
        rb_scr,
        colp,
    )


def _final_kernel(
    src_sm, slot_sm, k_hbm, tt_ref, c_ref, r_ref, al_out, ms_out, k_scr, ms_scr, t_ref, sems
):
    capacity = src_sm.shape[0]
    step = _chunk(capacity)
    copies = _chunk_copies(k_hbm, k_scr, sems, capacity)
    for copy in copies:
        copy.start()
    for o in range(t_ref.shape[0]):
        t_ref[o] = jnp.transpose(tt_ref[o])
    al_out[...] = jnp.zeros_like(al_out)
    ms_scr[...] = jnp.zeros_like(ms_scr)

    def body(t, carry):
        q = src_sm[t]
        o = slot_sm[t]
        kc = k_scr[t] * c_ref[o]
        al_out[q] += jnp.dot(kc, t_ref[o], precision=HIGH, preferred_element_type=jnp.float32)
        ms_scr[q] += kc
        return carry

    for part in range(capacity // step):
        copies[part].wait()
        lax.fori_loop(part * step, (part + 1) * step, body, 0, unroll=UNROLL)
    r = r_ref[...]
    al_out[...] = al_out[...] * r * math.sqrt(E)
    for q in range(ms_out.shape[0]):
        mass = jnp.broadcast_to(jnp.sum(ms_scr[q], axis=1, keepdims=True) * r_ref[q], (BLOCK, BLOCK))
        ms_out[q : q + 1, :] = jnp.transpose(mass)[0:1, :]


def _specs(n_smem, n_vmem):
    return [pl.BlockSpec(memory_space=pltpu.SMEM)] * n_smem + [
        pl.BlockSpec(memory_space=pltpu.VMEM)
    ] * n_vmem


def _vmem_out(n):
    return (pl.BlockSpec(memory_space=pltpu.VMEM),) * n


_ANY = pl.BlockSpec(memory_space=pl.ANY)


def first_sweep(tile_source, tile_slot, live, source_unit, fetched_t, rows_n):
    capacity = tile_source.shape[0]
    sb = source_unit.shape[0]
    slots = fetched_t.shape[0]
    return pl.pallas_call(
        _first_kernel,
        out_shape=(
            jax.ShapeDtypeStruct((capacity, BLOCK, BLOCK), jnp.float32),
            jax.ShapeDtypeStruct((sb, BLOCK, 1), jnp.float32),
            jax.ShapeDtypeStruct((rows_n, slots, BLOCK), jnp.float32),
        ),
        in_specs=_specs(3, 2),
        out_specs=(_ANY,) + _vmem_out(2),
        scratch_shapes=[
            pltpu.VMEM((capacity, BLOCK, BLOCK), jnp.float32),
            pltpu.VMEM((sb, BLOCK, BLOCK), jnp.float32),
            pltpu.VMEM((sb, BLOCK, BLOCK), jnp.float32),
            pltpu.VMEM((slots, 1, BLOCK), jnp.float32),
            pltpu.SemaphoreType.DMA((capacity // _chunk(capacity),)),
        ],
    )(tile_source, tile_slot, live, source_unit, fetched_t)


def again_sweep(tile_source, tile_slot, kernel, col, sb, rows_n):
    capacity = tile_source.shape[0]
    slots = col.shape[0]
    return pl.pallas_call(
        _again_kernel,
        out_shape=(
            jax.ShapeDtypeStruct((sb, BLOCK, 1), jnp.float32),
            jax.ShapeDtypeStruct((rows_n, slots, BLOCK), jnp.float32),
        ),
        in_specs=_specs(2, 0) + [_ANY] + _specs(0, 1),
        out_specs=_vmem_out(2),
        scratch_shapes=[
            pltpu.VMEM((capacity, BLOCK, BLOCK), jnp.float32),
            pltpu.VMEM((sb, BLOCK, BLOCK), jnp.float32),
            pltpu.VMEM((sb, BLOCK, BLOCK), jnp.float32),
            pltpu.VMEM((slots, 1, BLOCK), jnp.float32),
            pltpu.SemaphoreType.DMA((capacity // _chunk(capacity),)),
        ],
    )(tile_source, tile_slot, kernel, col)


def final(tile_source, tile_slot, kernel, fetched_t, col, row):
    capacity = tile_source.shape[0]
    sb = row.shape[0]
    slots = fetched_t.shape[0]
    return pl.pallas_call(
        _final_kernel,
        out_shape=(
            jax.ShapeDtypeStruct((sb, BLOCK, E), jnp.float32),
            jax.ShapeDtypeStruct((sb, BLOCK), jnp.float32),
        ),
        in_specs=_specs(2, 0) + [_ANY] + _specs(0, 3),
        out_specs=_vmem_out(2),
        scratch_shapes=[
            pltpu.VMEM((capacity, BLOCK, BLOCK), jnp.float32),
            pltpu.VMEM((sb, BLOCK, BLOCK), jnp.float32),
            pltpu.VMEM((slots, BLOCK, E), jnp.float32),
            pltpu.SemaphoreType.DMA((capacity // _chunk(capacity),)),
        ],
    )(tile_source, tile_slot, kernel, fetched_t, col, row)


def on_device(source_emb, target_emb, tile_source, tile_slot, tile_count, wanted):
    rows_n = lax.axis_size("rows")
    need = wanted.shape[1]
    target_blocks = target_emb.shape[0] // BLOCK
    slots = rows_n * need
    source_unit = unit_rows(source_emb).reshape(-1, BLOCK, E)
    owners = rows_n
    wanted_row = wanted.reshape(1, slots)
    wanted_all = lax.all_to_all(
        jnp.broadcast_to(wanted_row, (rows_n, slots)), "rows", split_axis=0, concat_axis=0, tiled=True
    )
    me = lax.axis_index("rows")
    asked = lax.dynamic_slice_in_dim(wanted_all, me * need, need, axis=1)
    own_unit_t = jnp.swapaxes(unit_rows(target_emb).reshape(target_blocks, BLOCK, E), 1, 2)
    outgoing = own_unit_t[asked.reshape(-1)]
    fetched_t = lax.all_to_all(outgoing, "rows", split_axis=0, concat_axis=0, tiled=True)
    same_block = (
        wanted_all.reshape(rows_n, owners, need, 1) == wanted.reshape(1, owners, 1, need)
    )[..., None]

    def column_scale_of(spread):
        gathered = lax.all_to_all(spread, "rows", split_axis=0, concat_axis=0, tiled=True)
        gathered = gathered.reshape(rows_n, owners, need, 1, BLOCK)
        totals = jnp.sum(jnp.where(same_block, gathered, 0.0), axis=(0, 2))
        return (1.0 / jnp.maximum(totals, COLUMN_FLOOR)).reshape(slots, 1, BLOCK)

    live = (jnp.arange(tile_source.shape[0]) < tile_count[0]).astype(jnp.float32)
    sb = source_unit.shape[0]
    fetched_t, same_block = lax.optimization_barrier((fetched_t, same_block))
    kernel, row, colp = first_sweep(tile_source, tile_slot, live, source_unit, fetched_t, rows_n)
    for iteration in range(1, ITERS):
        col = column_scale_of(colp)
        row, colp = again_sweep(tile_source, tile_slot, kernel, col, sb, rows_n)
    col = column_scale_of(colp)
    al, ms = final(tile_source, tile_slot, kernel, fetched_t, col, row)
    return (al.reshape(-1, E), ms.reshape(-1))


def solution(mesh):
    placed = (
        P(("groups", "rows"), None),
        P(("groups", "rows"), None),
        P(("groups", "rows")),
        P(("groups", "rows")),
        P(("groups", "rows")),
        P(("groups", "rows"), None),
    )
    return jax.shard_map(
        on_device,
        mesh=mesh,
        in_specs=placed,
        out_specs=(P(("groups", "rows"), None), P(("groups", "rows"))),
        check_vma=False,
    )
```

```python
import math

import jax
import jax.numpy as jnp
from jax import lax
from jax.experimental import pallas as pl
from jax.experimental.pallas import tpu as pltpu
from jax.sharding import PartitionSpec as P

E = 128
BLOCK = 128
ITERS = 2
UNROLL = 32

EPSILON = 1e-06
SOFTMAX_WARMTH = 0.03
ROW_MINIMUM = 1.0
COLUMN_FLOOR = 0.01
HIGHEST = lax.Precision.HIGHEST
HIGH = lax.Precision.HIGH

def unit_rows(values):
    return values * lax.rsqrt(jnp.sum(values * values, axis=-1, keepdims=True) + EPSILON)


def _tile(s_ref, tt_ref, q, o):
    cosine = jnp.dot(s_ref[q], tt_ref[o], precision=HIGHEST, preferred_element_type=jnp.float32)
    return jnp.exp(cosine / SOFTMAX_WARMTH)


def _bounds(capacity):
    step = math.gcd(capacity, 32)
    if step == 32 and capacity >= 64:
        return [0, 8] + list(range(32, capacity + 1, 32))
    return list(range(0, capacity + 1, step))


def _loop(lo, hi, body):
    lax.fori_loop(lo, hi, body, 0, unroll=min(UNROLL, hi - lo))


def _rows_cols(src_sm, slot_sm, tile_at, chunk_done, k_ref, c_ref, r_out, spread_out, acc, rb_scr, colp_out):
    capacity = src_sm.shape[0]
    sb = acc.shape[0]
    bounds = _bounds(capacity)
    acc[...] = jnp.zeros_like(acc)
    colp_out[...] = jnp.zeros_like(colp_out)

    def rows(t, carry):
        q = src_sm[t]
        o = slot_sm[t]
        if c_ref is None:
            acc[q] += tile_at(t, q, o)
        else:
            acc[q] += tile_at(t, q, o) * c_ref[o]
        return carry

    for part in range(len(bounds) - 1):
        chunk_done(part, "before")
        _loop(bounds[part], bounds[part + 1], rows)
        chunk_done(part, "after")
    for q in range(sb):
        r = 1.0 / jnp.maximum(jnp.sum(acc[q], axis=1, keepdims=True), ROW_MINIMUM)
        r_out[q] = r
        rb_scr[q] = jnp.broadcast_to(r, (BLOCK, BLOCK))

    def cols(t, carry):
        q = src_sm[t]
        o = slot_sm[t]
        colp_out[o] += jnp.sum(k_ref[t] * rb_scr[q], axis=0, keepdims=True)
        return carry

    lax.fori_loop(0, capacity, cols, 0, unroll=UNROLL)
    partials = jnp.concatenate([colp_out[o] for o in range(colp_out.shape[0])], axis=0)
    for d in range(spread_out.shape[0]):
        spread_out[d] = partials


def _chunk_copies(src, dst, sems, capacity):
    bounds = _bounds(capacity)
    return [
        pltpu.make_async_copy(
            src.at[pl.ds(lo, hi - lo)], dst.at[pl.ds(lo, hi - lo)], sems.at[part]
        )
        for part, (lo, hi) in enumerate(zip(bounds[:-1], bounds[1:]))
    ]


def _first_kernel(
    src_sm, slot_sm, live_ref, s_ref, tt_ref, k_hbm, r_out, spread_out, k_scr, acc, rb_scr, colp, sems
):
    capacity = src_sm.shape[0]
    copies = _chunk_copies(k_scr, k_hbm, sems, capacity)

    def build(t, q, o):
        k = _tile(s_ref, tt_ref, q, o) * live_ref[t]
        k_scr[t] = k
        return k

    def chunk_done(part, when):
        if when == "after":
            copies[part].start()

    _rows_cols(src_sm, slot_sm, build, chunk_done, k_scr, None, r_out, spread_out, acc, rb_scr, colp)
    for copy in copies:
        copy.wait()


def _again_kernel(src_sm, slot_sm, k_hbm, c_ref, r_out, spread_out, k_scr, acc, rb_scr, colp, sems):
    capacity = src_sm.shape[0]
    copies = _chunk_copies(k_hbm, k_scr, sems, capacity)
    for copy in copies:
        copy.start()

    def chunk_done(part, when):
        if when == "before":
            copies[part].wait()

    _rows_cols(
        src_sm,
        slot_sm,
        lambda t, q, o: k_scr[t],
        chunk_done,
        k_scr,
        c_ref,
        r_out,
        spread_out,
        acc,
        rb_scr,
        colp,
    )


def _final_kernel(
    src_sm, slot_sm, k_hbm, tt_ref, c_ref, r_ref, al_out, ms_out, k_scr, ms_scr, t_ref, sems
):
    capacity = src_sm.shape[0]
    bounds = _bounds(capacity)
    copies = _chunk_copies(k_hbm, k_scr, sems, capacity)
    for copy in copies:
        copy.start()
    for o in range(t_ref.shape[0]):
        t_ref[o] = jnp.transpose(tt_ref[o])
    al_out[...] = jnp.zeros_like(al_out)
    ms_scr[...] = jnp.zeros_like(ms_scr)

    def body(t, carry):
        q = src_sm[t]
        o = slot_sm[t]
        kc = k_scr[t] * c_ref[o]
        al_out[q] += jnp.dot(kc, t_ref[o], precision=HIGH, preferred_element_type=jnp.float32)
        ms_scr[q] += kc
        return carry

    for part in range(len(bounds) - 1):
        copies[part].wait()
        _loop(bounds[part], bounds[part + 1], body)
    r = r_ref[...]
    al_out[...] = al_out[...] * r * math.sqrt(E)
    for q in range(ms_out.shape[0]):
        mass = jnp.broadcast_to(jnp.sum(ms_scr[q], axis=1, keepdims=True) * r_ref[q], (BLOCK, BLOCK))
        ms_out[q : q + 1, :] = jnp.transpose(mass)[0:1, :]


def _specs(n_smem, n_vmem):
    return [pl.BlockSpec(memory_space=pltpu.SMEM)] * n_smem + [
        pl.BlockSpec(memory_space=pltpu.VMEM)
    ] * n_vmem


def _vmem_out(n):
    return (pl.BlockSpec(memory_space=pltpu.VMEM),) * n


_ANY = pl.BlockSpec(memory_space=pl.ANY)


def first_sweep(tile_source, tile_slot, live, source_unit, fetched_t, rows_n):
    capacity = tile_source.shape[0]
    sb = source_unit.shape[0]
    slots = fetched_t.shape[0]
    return pl.pallas_call(
        _first_kernel,
        out_shape=(
            jax.ShapeDtypeStruct((capacity, BLOCK, BLOCK), jnp.float32),
            jax.ShapeDtypeStruct((sb, BLOCK, 1), jnp.float32),
            jax.ShapeDtypeStruct((rows_n, slots, BLOCK), jnp.float32),
        ),
        in_specs=_specs(3, 2),
        out_specs=(_ANY,) + _vmem_out(2),
        scratch_shapes=[
            pltpu.VMEM((capacity, BLOCK, BLOCK), jnp.float32),
            pltpu.VMEM((sb, BLOCK, BLOCK), jnp.float32),
            pltpu.VMEM((sb, BLOCK, BLOCK), jnp.float32),
            pltpu.VMEM((slots, 1, BLOCK), jnp.float32),
            pltpu.SemaphoreType.DMA((len(_bounds(capacity)) - 1,)),
        ],
    )(tile_source, tile_slot, live, source_unit, fetched_t)


def again_sweep(tile_source, tile_slot, kernel, col, sb, rows_n):
    capacity = tile_source.shape[0]
    slots = col.shape[0]
    return pl.pallas_call(
        _again_kernel,
        out_shape=(
            jax.ShapeDtypeStruct((sb, BLOCK, 1), jnp.float32),
            jax.ShapeDtypeStruct((rows_n, slots, BLOCK), jnp.float32),
        ),
        in_specs=_specs(2, 0) + [_ANY] + _specs(0, 1),
        out_specs=_vmem_out(2),
        scratch_shapes=[
            pltpu.VMEM((capacity, BLOCK, BLOCK), jnp.float32),
            pltpu.VMEM((sb, BLOCK, BLOCK), jnp.float32),
            pltpu.VMEM((sb, BLOCK, BLOCK), jnp.float32),
            pltpu.VMEM((slots, 1, BLOCK), jnp.float32),
            pltpu.SemaphoreType.DMA((len(_bounds(capacity)) - 1,)),
        ],
    )(tile_source, tile_slot, kernel, col)


def final(tile_source, tile_slot, kernel, fetched_t, col, row):
    capacity = tile_source.shape[0]
    sb = row.shape[0]
    slots = fetched_t.shape[0]
    return pl.pallas_call(
        _final_kernel,
        out_shape=(
            jax.ShapeDtypeStruct((sb, BLOCK, E), jnp.float32),
            jax.ShapeDtypeStruct((sb, BLOCK), jnp.float32),
        ),
        in_specs=_specs(2, 0) + [_ANY] + _specs(0, 3),
        out_specs=_vmem_out(2),
        scratch_shapes=[
            pltpu.VMEM((capacity, BLOCK, BLOCK), jnp.float32),
            pltpu.VMEM((sb, BLOCK, BLOCK), jnp.float32),
            pltpu.VMEM((slots, BLOCK, E), jnp.float32),
            pltpu.SemaphoreType.DMA((len(_bounds(capacity)) - 1,)),
        ],
    )(tile_source, tile_slot, kernel, fetched_t, col, row)


def on_device(source_emb, target_emb, tile_source, tile_slot, tile_count, wanted):
    rows_n = lax.axis_size("rows")
    need = wanted.shape[1]
    target_blocks = target_emb.shape[0] // BLOCK
    slots = rows_n * need
    source_unit = unit_rows(source_emb).reshape(-1, BLOCK, E)
    owners = rows_n
    wanted_row = wanted.reshape(1, slots)
    wanted_all = lax.all_to_all(
        jnp.broadcast_to(wanted_row, (rows_n, slots)), "rows", split_axis=0, concat_axis=0, tiled=True
    )
    me = lax.axis_index("rows")
    asked = lax.dynamic_slice_in_dim(wanted_all, me * need, need, axis=1)
    own_unit_t = jnp.swapaxes(unit_rows(target_emb).reshape(target_blocks, BLOCK, E), 1, 2)
    outgoing = own_unit_t[asked.reshape(-1)]
    fetched_t = lax.all_to_all(outgoing, "rows", split_axis=0, concat_axis=0, tiled=True)
    same_block = (
        wanted_all.reshape(rows_n, owners, need, 1) == wanted.reshape(1, owners, 1, need)
    )[..., None]

    def column_scale_of(spread):
        gathered = lax.all_to_all(spread, "rows", split_axis=0, concat_axis=0, tiled=True)
        gathered = gathered.reshape(rows_n, owners, need, 1, BLOCK)
        totals = jnp.sum(jnp.where(same_block, gathered, 0.0), axis=(0, 2))
        return (1.0 / jnp.maximum(totals, COLUMN_FLOOR)).reshape(slots, 1, BLOCK)

    live = (jnp.arange(tile_source.shape[0]) < tile_count[0]).astype(jnp.float32)
    sb = source_unit.shape[0]
    fetched_t, same_block = lax.optimization_barrier((fetched_t, same_block))
    kernel, row, colp = first_sweep(tile_source, tile_slot, live, source_unit, fetched_t, rows_n)
    for iteration in range(1, ITERS):
        col = column_scale_of(colp)
        row, colp = again_sweep(tile_source, tile_slot, kernel, col, sb, rows_n)
    col = column_scale_of(colp)
    al, ms = final(tile_source, tile_slot, kernel, fetched_t, col, row)
    return (al.reshape(-1, E), ms.reshape(-1))


def solution(mesh):
    placed = (
        P(("groups", "rows"), None),
        P(("groups", "rows"), None),
        P(("groups", "rows")),
        P(("groups", "rows")),
        P(("groups", "rows")),
        P(("groups", "rows"), None),
    )
    return jax.shard_map(
        on_device,
        mesh=mesh,
        in_specs=placed,
        out_specs=(P(("groups", "rows"), None), P(("groups", "rows"))),
        check_vma=False,
    )
```

```python
import math

import jax
import jax.numpy as jnp
from jax import lax
from jax.experimental import pallas as pl
from jax.experimental.pallas import tpu as pltpu
from jax.sharding import PartitionSpec as P

E = 128
BLOCK = 128
ITERS = 2
UNROLL = 32

EPSILON = 1e-06
SOFTMAX_WARMTH = 0.03
ROW_MINIMUM = 1.0
COLUMN_FLOOR = 0.01
HIGHEST = lax.Precision.HIGHEST
HIGH = lax.Precision.HIGH

def unit_rows(values):
    return values * lax.rsqrt(jnp.sum(values * values, axis=-1, keepdims=True) + EPSILON)


def _tile(s_ref, tt_ref, q, o):
    cosine = jnp.dot(s_ref[q], tt_ref[o], precision=HIGHEST, preferred_element_type=jnp.float32)
    return jnp.exp(cosine / SOFTMAX_WARMTH)


def _bounds(capacity):
    step = math.gcd(capacity, 32)
    if step == 32 and capacity >= 64:
        return [0, 8] + list(range(32, capacity + 1, 32))
    return list(range(0, capacity + 1, step))


def _loop(lo, hi, body):
    lax.fori_loop(lo, hi, body, 0, unroll=min(UNROLL, hi - lo))


def _rows_cols(src_sm, slot_sm, tile_at, chunk_done, k_ref, c_ref, r_out, spread_out, acc, rb_scr, colp_out):
    capacity = src_sm.shape[0]
    sb = acc.shape[0]
    bounds = _bounds(capacity)
    acc[...] = jnp.zeros_like(acc)
    colp_out[...] = jnp.zeros_like(colp_out)

    def rows(t, carry):
        q = src_sm[t]
        o = slot_sm[t]
        if c_ref is None:
            acc[q] += tile_at(t, q, o)
        else:
            acc[q] += tile_at(t, q, o) * c_ref[o]
        return carry

    for part in range(len(bounds) - 1):
        chunk_done(part, "before")
        _loop(bounds[part], bounds[part + 1], rows)
        chunk_done(part, "after")
    for q in range(sb):
        r = 1.0 / jnp.maximum(jnp.sum(acc[q], axis=1, keepdims=True), ROW_MINIMUM)
        r_out[q] = r
        rb_scr[q] = jnp.broadcast_to(r, (BLOCK, BLOCK))

    def cols(t, carry):
        q = src_sm[t]
        o = slot_sm[t]
        colp_out[o] += jnp.sum(k_ref[t] * rb_scr[q], axis=0, keepdims=True)
        return carry

    lax.fori_loop(0, capacity, cols, 0, unroll=UNROLL)
    partials = jnp.concatenate([colp_out[o] for o in range(colp_out.shape[0])], axis=0)
    for d in range(spread_out.shape[0]):
        spread_out[d] = partials


def _column_scale(g_ref, m_ref, c_scr):
    totals = g_ref[0] * m_ref[0]
    for d in range(1, g_ref.shape[0]):
        totals = totals + g_ref[d] * m_ref[d]
    scale = 1.0 / jnp.maximum(totals, COLUMN_FLOOR)
    for o in range(c_scr.shape[0]):
        c_scr[o] = scale[o : o + 1, :]


def _chunk_copies(src, dst, sems, capacity):
    bounds = _bounds(capacity)
    return [
        pltpu.make_async_copy(
            src.at[pl.ds(lo, hi - lo)], dst.at[pl.ds(lo, hi - lo)], sems.at[part]
        )
        for part, (lo, hi) in enumerate(zip(bounds[:-1], bounds[1:]))
    ]


def _first_kernel(
    src_sm, slot_sm, live_ref, s_ref, tt_ref, k_hbm, r_out, spread_out, k_scr, acc, rb_scr, colp, sems
):
    capacity = src_sm.shape[0]
    copies = _chunk_copies(k_scr, k_hbm, sems, capacity)

    def build(t, q, o):
        k = _tile(s_ref, tt_ref, q, o) * live_ref[t]
        k_scr[t] = k
        return k

    def chunk_done(part, when):
        if when == "after":
            copies[part].start()

    _rows_cols(src_sm, slot_sm, build, chunk_done, k_scr, None, r_out, spread_out, acc, rb_scr, colp)
    for copy in copies:
        copy.wait()


def _again_kernel(
    src_sm, slot_sm, k_hbm, g_ref, m_ref, r_out, spread_out, k_scr, acc, rb_scr, colp, c_ref, sems
):
    capacity = src_sm.shape[0]
    copies = _chunk_copies(k_hbm, k_scr, sems, capacity)
    for copy in copies:
        copy.start()
    _column_scale(g_ref, m_ref, c_ref)

    def chunk_done(part, when):
        if when == "before":
            copies[part].wait()

    _rows_cols(
        src_sm,
        slot_sm,
        lambda t, q, o: k_scr[t],
        chunk_done,
        k_scr,
        c_ref,
        r_out,
        spread_out,
        acc,
        rb_scr,
        colp,
    )


def _final_kernel(
    src_sm, slot_sm, k_hbm, tt_ref, g_ref, m_ref, r_ref, al_out, ms_out, k_scr, ms_scr, t_ref, c_ref, sems
):
    capacity = src_sm.shape[0]
    bounds = _bounds(capacity)
    copies = _chunk_copies(k_hbm, k_scr, sems, capacity)
    for copy in copies:
        copy.start()
    _column_scale(g_ref, m_ref, c_ref)
    for o in range(t_ref.shape[0]):
        t_ref[o] = jnp.transpose(tt_ref[o])
    al_out[...] = jnp.zeros_like(al_out)
    ms_scr[...] = jnp.zeros_like(ms_scr)

    def body(t, carry):
        q = src_sm[t]
        o = slot_sm[t]
        kc = k_scr[t] * c_ref[o]
        al_out[q] += jnp.dot(kc, t_ref[o], precision=HIGH, preferred_element_type=jnp.float32)
        ms_scr[q] += kc
        return carry

    for part in range(len(bounds) - 1):
        copies[part].wait()
        _loop(bounds[part], bounds[part + 1], body)
    r = r_ref[...]
    al_out[...] = al_out[...] * r * math.sqrt(E)
    for q in range(ms_out.shape[0]):
        mass = jnp.broadcast_to(jnp.sum(ms_scr[q], axis=1, keepdims=True) * r_ref[q], (BLOCK, BLOCK))
        ms_out[q : q + 1, :] = jnp.transpose(mass)[0:1, :]


def _specs(n_smem, n_vmem):
    return [pl.BlockSpec(memory_space=pltpu.SMEM)] * n_smem + [
        pl.BlockSpec(memory_space=pltpu.VMEM)
    ] * n_vmem


def _vmem_out(n):
    return (pl.BlockSpec(memory_space=pltpu.VMEM),) * n


_ANY = pl.BlockSpec(memory_space=pl.ANY)


def first_sweep(tile_source, tile_slot, live, source_unit, fetched_t, rows_n):
    capacity = tile_source.shape[0]
    sb = source_unit.shape[0]
    slots = fetched_t.shape[0]
    return pl.pallas_call(
        _first_kernel,
        out_shape=(
            jax.ShapeDtypeStruct((capacity, BLOCK, BLOCK), jnp.float32),
            jax.ShapeDtypeStruct((sb, BLOCK, 1), jnp.float32),
            jax.ShapeDtypeStruct((rows_n, slots, BLOCK), jnp.float32),
        ),
        in_specs=_specs(3, 2),
        out_specs=(_ANY,) + _vmem_out(2),
        scratch_shapes=[
            pltpu.VMEM((capacity, BLOCK, BLOCK), jnp.float32),
            pltpu.VMEM((sb, BLOCK, BLOCK), jnp.float32),
            pltpu.VMEM((sb, BLOCK, BLOCK), jnp.float32),
            pltpu.VMEM((slots, 1, BLOCK), jnp.float32),
            pltpu.SemaphoreType.DMA((len(_bounds(capacity)) - 1,)),
        ],
    )(tile_source, tile_slot, live, source_unit, fetched_t)


def again_sweep(tile_source, tile_slot, kernel, col, sb, rows_n):
    capacity = tile_source.shape[0]
    slots = col[0].shape[1]
    return pl.pallas_call(
        _again_kernel,
        out_shape=(
            jax.ShapeDtypeStruct((sb, BLOCK, 1), jnp.float32),
            jax.ShapeDtypeStruct((rows_n, slots, BLOCK), jnp.float32),
        ),
        in_specs=_specs(2, 0) + [_ANY] + _specs(0, 2),
        out_specs=_vmem_out(2),
        scratch_shapes=[
            pltpu.VMEM((capacity, BLOCK, BLOCK), jnp.float32),
            pltpu.VMEM((sb, BLOCK, BLOCK), jnp.float32),
            pltpu.VMEM((sb, BLOCK, BLOCK), jnp.float32),
            pltpu.VMEM((slots, 1, BLOCK), jnp.float32),
            pltpu.VMEM((slots, 1, BLOCK), jnp.float32),
            pltpu.SemaphoreType.DMA((len(_bounds(capacity)) - 1,)),
        ],
    )(tile_source, tile_slot, kernel, *col)


def final(tile_source, tile_slot, kernel, fetched_t, col, row):
    capacity = tile_source.shape[0]
    sb = row.shape[0]
    slots = fetched_t.shape[0]
    return pl.pallas_call(
        _final_kernel,
        out_shape=(
            jax.ShapeDtypeStruct((sb, BLOCK, E), jnp.float32),
            jax.ShapeDtypeStruct((sb, BLOCK), jnp.float32),
        ),
        in_specs=_specs(2, 0) + [_ANY] + _specs(0, 4),
        out_specs=_vmem_out(2),
        scratch_shapes=[
            pltpu.VMEM((capacity, BLOCK, BLOCK), jnp.float32),
            pltpu.VMEM((sb, BLOCK, BLOCK), jnp.float32),
            pltpu.VMEM((slots, BLOCK, E), jnp.float32),
            pltpu.VMEM((slots, 1, BLOCK), jnp.float32),
            pltpu.SemaphoreType.DMA((len(_bounds(capacity)) - 1,)),
        ],
    )(tile_source, tile_slot, kernel, fetched_t, *col, row)


def on_device(source_emb, target_emb, tile_source, tile_slot, tile_count, wanted):
    rows_n = lax.axis_size("rows")
    need = wanted.shape[1]
    target_blocks = target_emb.shape[0] // BLOCK
    slots = rows_n * need
    source_unit = unit_rows(source_emb).reshape(-1, BLOCK, E)
    owners = rows_n
    wanted_row = wanted.reshape(1, slots)
    wanted_all = lax.all_to_all(
        jnp.broadcast_to(wanted_row, (rows_n, slots)), "rows", split_axis=0, concat_axis=0, tiled=True
    )
    me = lax.axis_index("rows")
    asked = lax.dynamic_slice_in_dim(wanted_all, me * need, need, axis=1)
    own_unit_t = jnp.swapaxes(unit_rows(target_emb).reshape(target_blocks, BLOCK, E), 1, 2)
    outgoing = own_unit_t[asked.reshape(-1)]
    fetched_t = lax.all_to_all(outgoing, "rows", split_axis=0, concat_axis=0, tiled=True)
    same_block = (
        wanted_all.reshape(rows_n, owners, need, 1) == wanted.reshape(1, owners, 1, need)
    )[..., None]

    def column_scale_of(spread):
        gathered = lax.all_to_all(spread, "rows", split_axis=0, concat_axis=0, tiled=True)
        if need == 1:
            return gathered, same_block.reshape(rows_n, slots, 1).astype(jnp.float32)
        gathered = gathered.reshape(rows_n, owners, need, 1, BLOCK)
        totals = jnp.sum(jnp.where(same_block, gathered, 0.0), axis=(0, 2))
        return totals.reshape(1, slots, BLOCK), jnp.ones((1, slots, 1), jnp.float32)

    live = (jnp.arange(tile_source.shape[0]) < tile_count[0]).astype(jnp.float32)
    sb = source_unit.shape[0]
    fetched_t, same_block = lax.optimization_barrier((fetched_t, same_block))
    kernel, row, colp = first_sweep(tile_source, tile_slot, live, source_unit, fetched_t, rows_n)
    for iteration in range(1, ITERS):
        col = column_scale_of(colp)
        row, colp = again_sweep(tile_source, tile_slot, kernel, col, sb, rows_n)
    col = column_scale_of(colp)
    al, ms = final(tile_source, tile_slot, kernel, fetched_t, col, row)
    return (al.reshape(-1, E), ms.reshape(-1))


def solution(mesh):
    placed = (
        P(("groups", "rows"), None),
        P(("groups", "rows"), None),
        P(("groups", "rows")),
        P(("groups", "rows")),
        P(("groups", "rows")),
        P(("groups", "rows"), None),
    )
    return jax.shard_map(
        on_device,
        mesh=mesh,
        in_specs=placed,
        out_specs=(P(("groups", "rows"), None), P(("groups", "rows"))),
        check_vma=False,
    )
```

```python
import math

import jax
import jax.numpy as jnp
from jax import lax
from jax.experimental import pallas as pl
from jax.experimental.pallas import tpu as pltpu
from jax.sharding import PartitionSpec as P

E = 128
BLOCK = 128
ITERS = 2
UNROLL = 32

EPSILON = 1e-06
SOFTMAX_WARMTH = 0.03
ROW_MINIMUM = 1.0
COLUMN_FLOOR = 0.01
HIGHEST = lax.Precision.HIGHEST
HIGH = lax.Precision.HIGH

def unit_rows(values):
    return values * lax.rsqrt(jnp.sum(values * values, axis=-1, keepdims=True) + EPSILON)


def _tile(s_ref, tt_ref, q, o):
    cosine = jnp.dot(s_ref[q], tt_ref[o], precision=HIGHEST, preferred_element_type=jnp.float32)
    return jnp.exp(cosine * (1.0 / SOFTMAX_WARMTH))


def _chunk(capacity):
    return math.gcd(capacity, 32)


def _rows_cols(src_sm, slot_sm, tile_at, chunk_done, k_ref, c_ref, r_out, spread_out, acc, rb_scr, colp_out):
    capacity = src_sm.shape[0]
    sb = acc.shape[0]
    step = _chunk(capacity)
    acc[...] = jnp.zeros_like(acc)
    colp_out[...] = jnp.zeros_like(colp_out)

    def rows(t, carry):
        q = src_sm[t]
        o = slot_sm[t]
        if c_ref is None:
            acc[q] += tile_at(t, q, o)
        else:
            acc[q] += tile_at(t, q, o) * c_ref[o]
        return carry

    for part in range(capacity // step):
        chunk_done(part, "before")
        lax.fori_loop(part * step, (part + 1) * step, rows, 0, unroll=UNROLL)
        chunk_done(part, "after")
    for q in range(sb):
        r = 1.0 / jnp.maximum(jnp.sum(acc[q], axis=1, keepdims=True), ROW_MINIMUM)
        r_out[q] = r
        rb_scr[q] = jnp.broadcast_to(r, (BLOCK, BLOCK))

    def cols(t, carry):
        q = src_sm[t]
        o = slot_sm[t]
        colp_out[o] += jnp.sum(k_ref[t] * rb_scr[q], axis=0, keepdims=True)
        return carry

    lax.fori_loop(0, capacity, cols, 0, unroll=UNROLL)
    partials = jnp.concatenate([colp_out[o] for o in range(colp_out.shape[0])], axis=0)
    for d in range(spread_out.shape[0]):
        spread_out[d] = partials


def _chunk_copies(src, dst, sems, capacity):
    step = _chunk(capacity)
    return [
        pltpu.make_async_copy(
            src.at[pl.ds(part * step, step)], dst.at[pl.ds(part * step, step)], sems.at[part]
        )
        for part in range(capacity // step)
    ]


def _first_kernel(
    src_sm, slot_sm, live_ref, s_ref, tt_ref, k_hbm, r_out, spread_out, k_scr, acc, rb_scr, colp, sems
):
    capacity = src_sm.shape[0]
    copies = _chunk_copies(k_scr, k_hbm, sems, capacity)

    def build(t, q, o):
        k = _tile(s_ref, tt_ref, q, o) * live_ref[t]
        k_scr[t] = k
        return k

    def chunk_done(part, when):
        if when == "after":
            copies[part].start()

    _rows_cols(src_sm, slot_sm, build, chunk_done, k_scr, None, r_out, spread_out, acc, rb_scr, colp)
    for copy in copies:
        copy.wait()


def _again_kernel(src_sm, slot_sm, k_hbm, c_ref, r_out, spread_out, k_scr, acc, rb_scr, colp, sems):
    capacity = src_sm.shape[0]
    copies = _chunk_copies(k_hbm, k_scr, sems, capacity)
    for copy in copies:
        copy.start()

    def chunk_done(part, when):
        if when == "before":
            copies[part].wait()

    _rows_cols(
        src_sm,
        slot_sm,
        lambda t, q, o: k_scr[t],
        chunk_done,
        k_scr,
        c_ref,
        r_out,
        spread_out,
        acc,
        rb_scr,
        colp,
    )


def _final_kernel(
    src_sm, slot_sm, k_hbm, tt_ref, c_ref, r_ref, al_out, ms_out, k_scr, ms_scr, t_ref, sems
):
    capacity = src_sm.shape[0]
    step = _chunk(capacity)
    copies = _chunk_copies(k_hbm, k_scr, sems, capacity)
    for copy in copies:
        copy.start()
    for o in range(t_ref.shape[0]):
        t_ref[o] = jnp.transpose(tt_ref[o])
    al_out[...] = jnp.zeros_like(al_out)
    ms_scr[...] = jnp.zeros_like(ms_scr)

    def body(t, carry):
        q = src_sm[t]
        o = slot_sm[t]
        kc = k_scr[t] * c_ref[o]
        al_out[q] += jnp.dot(kc, t_ref[o], precision=HIGH, preferred_element_type=jnp.float32)
        ms_scr[q] += kc
        return carry

    for part in range(capacity // step):
        copies[part].wait()
        lax.fori_loop(part * step, (part + 1) * step, body, 0, unroll=UNROLL)
    r = r_ref[...]
    al_out[...] = al_out[...] * r * math.sqrt(E)
    for q in range(ms_out.shape[0]):
        mass = jnp.broadcast_to(jnp.sum(ms_scr[q], axis=1, keepdims=True) * r_ref[q], (BLOCK, BLOCK))
        ms_out[q : q + 1, :] = jnp.transpose(mass)[0:1, :]


def _specs(n_smem, n_vmem):
    return [pl.BlockSpec(memory_space=pltpu.SMEM)] * n_smem + [
        pl.BlockSpec(memory_space=pltpu.VMEM)
    ] * n_vmem


def _vmem_out(n):
    return (pl.BlockSpec(memory_space=pltpu.VMEM),) * n


_ANY = pl.BlockSpec(memory_space=pl.ANY)


def first_sweep(tile_source, tile_slot, live, source_unit, fetched_t, rows_n):
    capacity = tile_source.shape[0]
    sb = source_unit.shape[0]
    slots = fetched_t.shape[0]
    return pl.pallas_call(
        _first_kernel,
        out_shape=(
            jax.ShapeDtypeStruct((capacity, BLOCK, BLOCK), jnp.float32),
            jax.ShapeDtypeStruct((sb, BLOCK, 1), jnp.float32),
            jax.ShapeDtypeStruct((rows_n, slots, BLOCK), jnp.float32),
        ),
        in_specs=_specs(3, 2),
        out_specs=(_ANY,) + _vmem_out(2),
        scratch_shapes=[
            pltpu.VMEM((capacity, BLOCK, BLOCK), jnp.float32),
            pltpu.VMEM((sb, BLOCK, BLOCK), jnp.float32),
            pltpu.VMEM((sb, BLOCK, BLOCK), jnp.float32),
            pltpu.VMEM((slots, 1, BLOCK), jnp.float32),
            pltpu.SemaphoreType.DMA((capacity // _chunk(capacity),)),
        ],
    )(tile_source, tile_slot, live, source_unit, fetched_t)


def again_sweep(tile_source, tile_slot, kernel, col, sb, rows_n):
    capacity = tile_source.shape[0]
    slots = col.shape[0]
    return pl.pallas_call(
        _again_kernel,
        out_shape=(
            jax.ShapeDtypeStruct((sb, BLOCK, 1), jnp.float32),
            jax.ShapeDtypeStruct((rows_n, slots, BLOCK), jnp.float32),
        ),
        in_specs=_specs(2, 0) + [_ANY] + _specs(0, 1),
        out_specs=_vmem_out(2),
        scratch_shapes=[
            pltpu.VMEM((capacity, BLOCK, BLOCK), jnp.float32),
            pltpu.VMEM((sb, BLOCK, BLOCK), jnp.float32),
            pltpu.VMEM((sb, BLOCK, BLOCK), jnp.float32),
            pltpu.VMEM((slots, 1, BLOCK), jnp.float32),
            pltpu.SemaphoreType.DMA((capacity // _chunk(capacity),)),
        ],
    )(tile_source, tile_slot, kernel, col)


def final(tile_source, tile_slot, kernel, fetched_t, col, row):
    capacity = tile_source.shape[0]
    sb = row.shape[0]
    slots = fetched_t.shape[0]
    return pl.pallas_call(
        _final_kernel,
        out_shape=(
            jax.ShapeDtypeStruct((sb, BLOCK, E), jnp.float32),
            jax.ShapeDtypeStruct((sb, BLOCK), jnp.float32),
        ),
        in_specs=_specs(2, 0) + [_ANY] + _specs(0, 3),
        out_specs=_vmem_out(2),
        scratch_shapes=[
            pltpu.VMEM((capacity, BLOCK, BLOCK), jnp.float32),
            pltpu.VMEM((sb, BLOCK, BLOCK), jnp.float32),
            pltpu.VMEM((slots, BLOCK, E), jnp.float32),
            pltpu.SemaphoreType.DMA((capacity // _chunk(capacity),)),
        ],
    )(tile_source, tile_slot, kernel, fetched_t, col, row)


def on_device(source_emb, target_emb, tile_source, tile_slot, tile_count, wanted):
    rows_n = lax.axis_size("rows")
    need = wanted.shape[1]
    target_blocks = target_emb.shape[0] // BLOCK
    slots = rows_n * need
    source_unit = unit_rows(source_emb).reshape(-1, BLOCK, E)
    owners = rows_n
    wanted_row = wanted.reshape(1, slots)
    wanted_all = lax.all_to_all(
        jnp.broadcast_to(wanted_row, (rows_n, slots)), "rows", split_axis=0, concat_axis=0, tiled=True
    )
    me = lax.axis_index("rows")
    asked = lax.dynamic_slice_in_dim(wanted_all, me * need, need, axis=1)
    own_unit_t = jnp.swapaxes(unit_rows(target_emb).reshape(target_blocks, BLOCK, E), 1, 2)
    outgoing = own_unit_t[asked.reshape(-1)]
    fetched_t = lax.all_to_all(outgoing, "rows", split_axis=0, concat_axis=0, tiled=True)
    same_block = (
        wanted_all.reshape(rows_n, owners, need, 1) == wanted.reshape(1, owners, 1, need)
    )[..., None]

    def column_scale_of(spread):
        gathered = lax.all_to_all(spread, "rows", split_axis=0, concat_axis=0, tiled=True)
        gathered = gathered.reshape(rows_n, owners, need, 1, BLOCK)
        totals = jnp.sum(jnp.where(same_block, gathered, 0.0), axis=(0, 2))
        return (1.0 / jnp.maximum(totals, COLUMN_FLOOR)).reshape(slots, 1, BLOCK)

    live = (jnp.arange(tile_source.shape[0]) < tile_count[0]).astype(jnp.float32)
    sb = source_unit.shape[0]
    fetched_t, same_block = lax.optimization_barrier((fetched_t, same_block))
    kernel, row, colp = first_sweep(tile_source, tile_slot, live, source_unit, fetched_t, rows_n)
    for iteration in range(1, ITERS):
        col = column_scale_of(colp)
        row, colp = again_sweep(tile_source, tile_slot, kernel, col, sb, rows_n)
    col = column_scale_of(colp)
    al, ms = final(tile_source, tile_slot, kernel, fetched_t, col, row)
    return (al.reshape(-1, E), ms.reshape(-1))


def solution(mesh):
    placed = (
        P(("groups", "rows"), None),
        P(("groups", "rows"), None),
        P(("groups", "rows")),
        P(("groups", "rows")),
        P(("groups", "rows")),
        P(("groups", "rows"), None),
    )
    return jax.shard_map(
        on_device,
        mesh=mesh,
        in_specs=placed,
        out_specs=(P(("groups", "rows"), None), P(("groups", "rows"))),
        check_vma=False,
    )
```
